256 devices in a mesh: ctx: 32 (over x, y, core), tp: 8 (over z).
Axes of the slice: x: 4, y: 4, z: 8, core: 2. Of those that a mesh axis runs over, the one named last changes fastest.
Arguments:
- hidden_states: bfloat16 [65536, 4096], P('ctx', 'tp')
- chosen: int32 [12288], P('ctx'), may hold values from 0 to 2048, as said below
- router_gate: float32 [12288], P('ctx'), may hold values from 0.2 to 1
- w_query: bfloat16 [4096, 4096], P(None, 'tp'), may hold values from -0.09375 to 0.09375
- w_key: bfloat16 [4096, 1024], P(None, 'tp'), may hold values from -0.09375 to 0.09375
- w_value: bfloat16 [4096, 1024], P(None, 'tp'), may hold values from -0.09375 to 0.09375
Outputs:
- attended: bfloat16 [12288, 4096], P('ctx', 'tp')
The draws below stay inside these ranges and needn't reach their ends.
Inputs may be any that keep to these rules, and one draw needn't show every extreme that they name: `chosen`: each shard's 384 slots hold the sorted distinct positions of its routed tokens, then 2048 in every unused slot; a shard routes from 128 to 384 tokens, some shard exactly 384, and all shards together 65536 // 8.
All inputs are finite; a program needn't handle non-finite values.
Results may differ from the reference program's by a relative error of at most 0.035.
Values may be sent and summed in bfloat16 or wider, within the bound.
No kernel may reach another device: no remote copies, remote signals or barrier semaphores. Data moves between devices by JAX's collectives and lax.ppermute only.
A program may use at most 64 MiB of HBM per device.

```python
import math
import jax
import jax.numpy as jnp
from jax import lax

D = 4096
QHEADS = 32
KV_HEADS = 8
HEAD_DIM = 128
SEQ_DEV = 2048
SEL_AVG = 256
SKEW = 128
CAP = 384
TOKENS = 65536
SLOTS = 12288


def shard_counts(key):
    shards = SLOTS // CAP
    first_key, second_key = jax.random.split(jax.random.fold_in(key, 7))
    order = jax.random.permutation(first_key, shards)
    offsets = jax.random.randint(second_key, (shards // 2,), 0, SKEW + 1)
    offsets = offsets.at[0].set(SKEW)
    paired = jnp.stack([SEL_AVG + offsets, SEL_AVG - offsets], axis=1).reshape(-1).astype(jnp.int32)
    return jnp.zeros((shards,), jnp.int32).at[order].set(paired)


def draw_chosen(key, part):
    shards = SLOTS // CAP
    counts = shard_counts(key)
    shard_keys = jax.random.split(jax.random.fold_in(key, 11), shards)

    def one_shard(shard_key, count):
        shuffled = jax.random.permutation(shard_key, SEQ_DEV)[:CAP].astype(jnp.int32)
        used = jnp.arange(CAP, dtype=jnp.int32) < count
        return jnp.sort(jnp.where(used, shuffled, SEQ_DEV))
    return jax.vmap(one_shard)(shard_keys, counts).reshape(-1).astype(jnp.int32)


def draw_hidden_states(key, part):
    first_key = jax.random.fold_in(jax.random.fold_in(key, 3), 0)
    values_out = jnp.clip(jax.random.normal(first_key, (TOKENS, D), jnp.float32), -6.0, 6.0)
    return values_out.astype(jnp.bfloat16)


def block_levels(own_key, dims, pieces, smallest, top_value):
    level, own = 1.0, jax.random.fold_in(own_key, 6)
    for dim, blocks in pieces:
        steps = jnp.exp(jax.random.uniform(jax.random.fold_in(own, dim), (blocks,), jnp.float32, smallest / len(pieces), top_value / len(pieces)))
        level = level * jnp.repeat(steps, dims[dim] // blocks).reshape([-1 if axis == dim else 1 for axis in range(len(dims))])
    return level


def scatter_about(stream_key, shape, deviation, limit, cuts=(), kind=jnp.bfloat16):
    entries = deviation * jax.random.normal(stream_key, shape, jnp.float32)
    if cuts:
        entries = entries * block_levels(stream_key, shape, cuts, -0.22, 0.18)
    return jnp.clip(entries, -limit, limit).astype(kind)


def setup_inputs(seed: int = 0) -> dict:
    arg_keys = jax.random.split(jax.random.key(seed), 7)
    hidden_states = draw_hidden_states(jax.random.fold_in(arg_keys[6], 71), 0)
    chosen = draw_chosen(jax.random.fold_in(arg_keys[6], 71), 0)
    router_gate = jnp.clip(jnp.exp(math.log(1.0) - 1.609438 * jax.random.uniform(arg_keys[2], (SLOTS,), jnp.float32) ** block_levels(arg_keys[2], (SLOTS,), ((0, 32),), -0.2, 0.2)), 0.2, 1.0)
    w_query = scatter_about(arg_keys[3], (D, QHEADS * HEAD_DIM), D ** -0.5, 0.09375, ((1, 8),))
    w_key = scatter_about(arg_keys[4], (D, KV_HEADS * HEAD_DIM), D ** -0.5, 0.09375, ((1, 8),))
    w_value = scatter_about(arg_keys[5], (D, KV_HEADS * HEAD_DIM), D ** -0.5, 0.09375, ((1, 8),))
    return {"hidden_states": hidden_states, "chosen": chosen, "router_gate": router_gate, "w_query": w_query, "w_key": w_key, "w_value": w_value}


ROPE_BASE = 500000.0


def rotate(values_in, position):
    half_dim = values_in.shape[-1] // 2
    frequency = jnp.exp(jnp.arange(half_dim, dtype=jnp.float32) * (-2.0 * math.log(ROPE_BASE) / values_in.shape[-1]))
    angles = position.astype(jnp.float32)[:, None] * frequency[None, :]
    cosine = jnp.cos(angles)[:, None, :]
    sine = jnp.sin(angles)[:, None, :]
    first = values_in[..., :half_dim]
    second = values_in[..., half_dim:]
    return jnp.concatenate([first * cosine - second * sine, second * cosine + first * sine], axis=-1)


def reference(hidden_states, chosen, router_gate, w_query, w_key, w_value):
    shards = SLOTS // CAP
    local_pos = chosen.reshape(shards, CAP)
    live = local_pos < SEQ_DEV
    shard_base = (jnp.arange(shards, dtype=jnp.int32) * SEQ_DEV)[:, None]
    token_rows = (shard_base + jnp.minimum(local_pos, SEQ_DEV - 1)).reshape(-1).astype(jnp.int32)
    position = jnp.where(live, shard_base + local_pos, TOKENS + 1).reshape(-1).astype(jnp.int32)
    picked = hidden_states[token_rows]
    group = QHEADS // KV_HEADS
    query = jnp.dot(picked, w_query, preferred_element_type=jnp.float32).reshape(SLOTS, QHEADS, HEAD_DIM)
    query = (rotate(query, position) * HEAD_DIM ** -0.5).astype(jnp.bfloat16)
    query = query.reshape(shards, CAP, KV_HEADS, group, HEAD_DIM)
    key_all = jnp.dot(picked, w_key, preferred_element_type=jnp.float32).reshape(SLOTS, KV_HEADS, HEAD_DIM)
    key_all = rotate(key_all, position).astype(jnp.bfloat16)
    value_all = jnp.dot(picked, w_value, preferred_element_type=jnp.float32).astype(jnp.bfloat16)
    value_all = value_all.reshape(SLOTS, KV_HEADS, HEAD_DIM)
    query_pos = position.reshape(shards, CAP)

    def per_head(packed):
        key_head, value_head, query_head = packed

        def per_block(inner):
            query_block, block_pos = inner
            scores = jnp.einsum("rgd,kd->grk", query_block.astype(jnp.float32), key_head.astype(jnp.float32))
            allowed = position[None, None, :] <= block_pos[None, :, None]
            largest = jnp.max(jnp.where(allowed, scores, -jnp.inf), axis=-1, keepdims=True)
            weights = jnp.where(allowed, jnp.exp(scores - largest), 0.0)
            totals = jnp.sum(weights, axis=-1)
            weights_b = weights.astype(jnp.bfloat16).astype(jnp.float32)
            mixed = jnp.einsum("grk,kd->rgd", weights_b, value_head.astype(jnp.float32))
            return mixed / jnp.transpose(totals)[:, :, None]

        return lax.map(per_block, (query_head, query_pos))

    heads_out = lax.map(per_head, (jnp.transpose(key_all, (1, 0, 2)), jnp.transpose(value_all, (1, 0, 2)), jnp.transpose(query, (2, 0, 1, 3, 4))))
    context = jnp.transpose(heads_out, (1, 2, 0, 3, 4)).reshape(SLOTS, QHEADS * HEAD_DIM)
    gated = jnp.where(live.reshape(-1), router_gate, 0.0)
    return (context * gated[:, None]).astype(jnp.bfloat16)
```

```python
import math

import jax
import jax.numpy as jnp
from jax import lax
from jax.sharding import PartitionSpec as P

HEAD_DIM = 128


ROPE_BASE = 500000.0
MASKED = -1e30


def rotate(values_in, position):
    half_dim = values_in.shape[-1] // 2
    frequency = jnp.exp(
        jnp.arange(half_dim, dtype=jnp.float32) * (-2.0 * math.log(ROPE_BASE) / values_in.shape[-1])
    )
    angles = position.astype(jnp.float32)[:, None] * frequency[None, :]
    cosine = jnp.cos(angles)[:, None, :]
    sine = jnp.sin(angles)[:, None, :]
    first = values_in[..., :half_dim]
    second = values_in[..., half_dim:]
    return jnp.concatenate(
        [first * cosine - second * sine, second * cosine + first * sine], axis=-1
    )


def empty_state(count, kv_local, group, head_dim):
    return (
        jnp.full((kv_local, group, count), MASKED, jnp.float32),
        jnp.zeros((kv_local, group, count), jnp.float32),
        jnp.zeros((count, kv_local, group, head_dim), jnp.float32),
    )


def update(state, queries, query_pos, key_block, value_block, key_pos):
    running, totals, summed = state
    scores = jnp.einsum("rhgd,khd->hgrk", queries, key_block, preferred_element_type=jnp.float32)
    allowed = key_pos[None, None, None, :] <= query_pos[None, None, :, None]
    newest = jnp.maximum(running, jnp.max(jnp.where(allowed, scores, MASKED), axis=-1))
    factor = jnp.exp(running - newest)
    weights = jnp.where(allowed, jnp.exp(scores - newest[..., None]), 0.0)
    totals = totals * factor + jnp.sum(weights, axis=-1)
    mixed = jnp.einsum(
        "hgrk,khd->rhgd",
        weights.astype(jnp.bfloat16),
        value_block,
        preferred_element_type=jnp.float32,
    )
    summed = summed * jnp.transpose(factor, (2, 0, 1))[..., None] + mixed
    return (newest, totals, summed)


def finish(state):
    running, totals, summed = state
    denom = jnp.where(totals > 0.0, totals, 1.0)
    return summed / jnp.transpose(denom, (2, 0, 1))[..., None]


def highest(position, pad_mark):
    return jnp.max(jnp.where(position < pad_mark, position, -1))


def fold_keys(states, pieces, groups):
    key_rows, value_rows, key_pos = pieces
    length = key_rows.shape[0]
    block_rows = length
    for size_rows in (1536, 768, 384):
        block_rows = size_rows
        break
    blocks = length // block_rows
    shaped = (
        key_rows.reshape((blocks, block_rows) + key_rows.shape[1:]),
        value_rows.reshape((blocks, block_rows) + value_rows.shape[1:]),
        key_pos.reshape(blocks, block_rows),
    )

    def advance(carried, block):
        key_block, value_block, block_pos = block
        fresh = []
        for state, group_data in zip(carried, groups):
            queries, query_pos, limit = group_data

            def visit(current):
                return update(current, queries, query_pos, key_block, value_block, block_pos)

            def keep_state(current):
                return current

            fresh.append(lax.cond(jnp.min(block_pos) > limit, keep_state, visit, state))
        return (tuple(fresh), None)

    result, unused = lax.scan(advance, tuple(states), shaped)
    return result


CODE_BASE = 64
EXTRA_ROWS = 16


def pack_payload(key_rows, value_rows, chosen):
    slot_count = chosen.shape[0]
    width = key_rows.shape[1] * key_rows.shape[2]
    rows = jnp.concatenate(
        [key_rows.reshape(slot_count, width), value_rows.reshape(slot_count, width)], axis=1
    )
    digits = jnp.concatenate(
        [(chosen // CODE_BASE).reshape(-1, width), (chosen % CODE_BASE).reshape(-1, width)], axis=1
    ).astype(jnp.bfloat16)
    pad = jnp.zeros((EXTRA_ROWS - digits.shape[0], 2 * width), jnp.bfloat16)
    return jnp.concatenate([rows, digits, pad], axis=0)


def unpack_payload(payload, shards, slot_count, kv_local, head_dim):
    width = kv_local * head_dim
    blocks = payload.reshape(shards, slot_count + EXTRA_ROWS, 2 * width)
    key_all = blocks[:, :slot_count, :width].reshape(shards * slot_count, kv_local, head_dim)
    value_all = blocks[:, :slot_count, width:].reshape(shards * slot_count, kv_local, head_dim)
    code_rows = slot_count // width
    digits = blocks[:, slot_count : slot_count + code_rows, :].astype(jnp.int32)
    chosen_all = digits[:, :, :width] * CODE_BASE + digits[:, :, width:]
    return key_all, value_all, chosen_all.reshape(shards, slot_count)


def ring_project(picked, weights, axis):
    size = lax.axis_size(axis)
    idx = lax.axis_index(axis)
    width = picked.shape[1]
    forward = [(i, (i + 1) % size) for i in range(size)]
    backward = [(i, (i - 1) % size) for i in range(size)]

    def partial(block, source):
        start = source * width
        return [
            jnp.dot(block, lax.dynamic_slice_in_dim(w, start, width, axis=0), preferred_element_type=jnp.float32)
            for w in weights
        ]

    sums = partial(picked, idx)
    ahead = picked
    behind = picked
    steps_ahead = size // 2
    steps_behind = size - 1 - steps_ahead
    for step in range(1, steps_ahead + 1):
        ahead = lax.ppermute(ahead, axis, forward)
        parts = [partial(ahead, (idx - step) % size)]
        if step <= steps_behind:
            behind = lax.ppermute(behind, axis, backward)
            parts.append(partial(behind, (idx + step) % size))
        for part in parts:
            sums = [s + p for s, p in zip(sums, part)]
    return sums


def body(hidden_states, chosen, router_gate, w_query, w_key, w_value):
    seq_rows = hidden_states.shape[0]
    slot_count = chosen.shape[0]
    head_dim = HEAD_DIM
    query_width = w_query.shape[1]
    kv_width = w_key.shape[1]
    kv_local = kv_width // head_dim
    heads_local = query_width // head_dim
    group = heads_local // kv_local
    shards = lax.axis_size("ctx")
    live = chosen < seq_rows
    pad_mark = shards * seq_rows + 1
    position = jnp.where(live, lax.axis_index("ctx") * seq_rows + chosen, pad_mark)
    picked = hidden_states[jnp.minimum(chosen, seq_rows - 1)]
    gated = jnp.where(live, router_gate, 0.0)
    query_part, key_part, value_part = ring_project(picked, (w_query, w_key, w_value), "tp")
    queries = (
        rotate(query_part.reshape(slot_count, heads_local, head_dim), position) * head_dim ** (-0.5)
    ).astype(jnp.bfloat16)
    queries = queries.reshape(slot_count, kv_local, group, head_dim)
    key_rows = rotate(key_part.reshape(slot_count, kv_local, head_dim), position).astype(
        jnp.bfloat16
    )
    value_rows = value_part.reshape(slot_count, kv_local, head_dim).astype(jnp.bfloat16)
    payload = pack_payload(key_rows, value_rows, chosen)
    payload = lax.all_gather(payload, "ctx", axis=0, tiled=True)
    key_all, value_all, chosen_all = unpack_payload(payload, shards, slot_count, kv_local, head_dim)
    shard_base = (jnp.arange(shards, dtype=jnp.int32) * seq_rows)[:, None]
    key_pos = jnp.where(chosen_all < seq_rows, shard_base + chosen_all, pad_mark).reshape(-1)
    groups = [(queries, position, highest(position, pad_mark))]
    states = fold_keys(
        (empty_state(slot_count, kv_local, group, head_dim),),
        (key_all, value_all, key_pos),
        groups,
    )
    result = (finish(states[0]) * gated[:, None, None, None]).astype(jnp.bfloat16)
    return result.reshape(slot_count, query_width)


def solution(mesh):
    placed = (P("ctx", "tp"), P("ctx"), P("ctx"), P(None, "tp"), P(None, "tp"), P(None, "tp"))
    return jax.shard_map(
        body, mesh=mesh, in_specs=placed, out_specs=P("ctx", "tp"), check_vma=False
    )
```

```python
import functools
import math

import jax
import jax.numpy as jnp
from jax import lax
from jax.experimental import pallas as pl
from jax.experimental.pallas import tpu as pltpu
from jax.sharding import PartitionSpec as P

HEAD_DIM = 128


ROPE_BASE = 500000.0
MASKED = -1e30
SUB = 128


def rotate(values_in, position):
    half_dim = values_in.shape[-1] // 2
    frequency = jnp.exp(
        jnp.arange(half_dim, dtype=jnp.float32) * (-2.0 * math.log(ROPE_BASE) / values_in.shape[-1])
    )
    angles = position.astype(jnp.float32)[:, None] * frequency[None, :]
    cosine = jnp.cos(angles)[:, None, :]
    sine = jnp.sin(angles)[:, None, :]
    first = values_in[..., :half_dim]
    second = values_in[..., half_dim:]
    return jnp.concatenate(
        [first * cosine - second * sine, second * cosine + first * sine], axis=-1
    )


def attend_kernel(scalars, q_ref, qpos_ref, gate_ref, kv_ref, kpos_ref, out_ref, m_scr, l_scr, acc_scr, *, q_rows, group, shards):
    t = pl.program_id(0)
    own = scalars[0]
    q_blocks = scalars[1]
    key_blocks = (scalars[2 + t] + (SUB - 1)) // SUB
    rows = group * SUB
    head_dim = q_ref.shape[1]

    @pl.when(t == 0)
    def _():
        m_scr[...] = jnp.full(m_scr.shape, MASKED, jnp.float32)
        l_scr[...] = jnp.zeros(l_scr.shape, jnp.float32)
        acc_scr[...] = jnp.zeros(acc_scr.shape, jnp.float32)

    for qb in range(q_rows // rows):
        for kb in range(kv_ref.shape[0] // SUB):
            @pl.when((t <= own) & (qb < q_blocks) & (kb < key_blocks))
            def _():
                r0, k0 = qb * rows, kb * SUB
                q = q_ref[r0:r0 + rows, :]
                k = kv_ref[k0:k0 + SUB, :head_dim]
                v = kv_ref[k0:k0 + SUB, head_dim:]
                s = lax.dot_general(q, k, (((1,), (1,)), ((), ())), preferred_element_type=jnp.float32)
                allowed = kpos_ref[:, k0:k0 + SUB] <= qpos_ref[r0:r0 + rows, :]
                m_prev = m_scr[r0:r0 + rows, :]
                m_cur = jnp.max(jnp.where(allowed, s, MASKED), axis=1, keepdims=True)
                m_new = jnp.maximum(m_prev, m_cur)
                alpha = jnp.exp(m_prev - m_new)
                p = jnp.where(allowed, jnp.exp(s - m_new[:, :1]), 0.0)
                l_scr[r0:r0 + rows, :] = alpha * l_scr[r0:r0 + rows, :] + jnp.sum(p, axis=1, keepdims=True)
                acc_scr[r0:r0 + rows, :] = alpha[:, :1] * acc_scr[r0:r0 + rows, :] + jnp.dot(
                    p.astype(jnp.bfloat16), v, preferred_element_type=jnp.float32
                )
                m_scr[r0:r0 + rows, :] = m_new

    @pl.when(t == shards - 1)
    def _():
        total = l_scr[...]
        denom = jnp.where(total > 0.0, total, 1.0)
        out_ref[...] = ((acc_scr[...] / denom) * gate_ref[...]).astype(out_ref.dtype)


def attend(scalars, q, qpos, gate, kv, kpos, interpret=False):
    q_rows, head_dim = q.shape
    shards, _, width = kv.shape
    slots = kpos.shape[2]
    group = q_rows // (slots)
    kernel = functools.partial(attend_kernel, q_rows=q_rows, group=group, shards=shards)

    def key_map(t, sc):
        return (jnp.minimum(t, sc[0]), 0, 0)

    grid_spec = pltpu.PrefetchScalarGridSpec(
        num_scalar_prefetch=1,
        grid=(shards,),
        in_specs=[
            pl.BlockSpec((q_rows, head_dim), lambda t, sc: (0, 0)),
            pl.BlockSpec((q_rows, 1), lambda t, sc: (0, 0)),
            pl.BlockSpec((q_rows, 1), lambda t, sc: (0, 0)),
            pl.BlockSpec((None, slots, width), key_map),
            pl.BlockSpec((None, 1, slots), key_map),
        ],
        out_specs=pl.BlockSpec((q_rows, head_dim), lambda t, sc: (0, 0)),
        scratch_shapes=[
            pltpu.VMEM((q_rows, 128), jnp.float32),
            pltpu.VMEM((q_rows, 128), jnp.float32),
            pltpu.VMEM((q_rows, head_dim), jnp.float32),
        ],
    )
    return pl.pallas_call(
        kernel,
        grid_spec=grid_spec,
        out_shape=jax.ShapeDtypeStruct((q_rows, head_dim), jnp.bfloat16),
        compiler_params=pltpu.CompilerParams(dimension_semantics=("arbitrary",)),
        interpret=interpret,
    )(scalars, q, qpos, gate, kv, kpos)


CODE_BASE = 64
EXTRA_ROWS = 16


def pack_payload(key_rows, value_rows, chosen):
    slot_count = chosen.shape[0]
    width = key_rows.shape[1] * key_rows.shape[2]
    rows = jnp.concatenate(
        [key_rows.reshape(slot_count, width), value_rows.reshape(slot_count, width)], axis=1
    )
    digits = jnp.concatenate(
        [(chosen // CODE_BASE).reshape(-1, width), (chosen % CODE_BASE).reshape(-1, width)], axis=1
    ).astype(jnp.bfloat16)
    pad = jnp.zeros((EXTRA_ROWS - digits.shape[0], 2 * width), jnp.bfloat16)
    return jnp.concatenate([rows, digits, pad], axis=0)


def unpack_chosen(blocks, slot_count, width):
    code_rows = slot_count // width
    digits = blocks[:, slot_count : slot_count + code_rows, :].astype(jnp.int32)
    chosen_all = digits[:, :, :width] * CODE_BASE + digits[:, :, width:]
    return chosen_all.reshape(blocks.shape[0], slot_count)


def ring_project(picked, weights, axis):
    size = lax.axis_size(axis)
    idx = lax.axis_index(axis)
    width = picked.shape[1]
    forward = [(i, (i + 1) % size) for i in range(size)]
    backward = [(i, (i - 1) % size) for i in range(size)]

    def partial(block, source):
        start = source * width
        return [
            jnp.dot(block, lax.dynamic_slice_in_dim(w, start, width, axis=0), preferred_element_type=jnp.float32)
            for w in weights
        ]

    sums = partial(picked, idx)
    ahead = picked
    behind = picked
    steps_ahead = size // 2
    steps_behind = size - 1 - steps_ahead
    for step in range(1, steps_ahead + 1):
        ahead = lax.ppermute(ahead, axis, forward)
        parts = [partial(ahead, (idx - step) % size)]
        if step <= steps_behind:
            behind = lax.ppermute(behind, axis, backward)
            parts.append(partial(behind, (idx + step) % size))
        for part in parts:
            sums = [s + p for s, p in zip(sums, part)]
    return sums


def body(hidden_states, chosen, router_gate, w_query, w_key, w_value):
    seq_rows = hidden_states.shape[0]
    slot_count = chosen.shape[0]
    head_dim = HEAD_DIM
    query_width = w_query.shape[1]
    kv_width = w_key.shape[1]
    kv_local = kv_width // head_dim
    heads_local = query_width // head_dim
    group = heads_local // kv_local
    shards = lax.axis_size("ctx")
    live = chosen < seq_rows
    pad_mark = shards * seq_rows + 1
    position = jnp.where(live, lax.axis_index("ctx") * seq_rows + chosen, pad_mark)
    picked = hidden_states[jnp.minimum(chosen, seq_rows - 1)]
    gated = jnp.where(live, router_gate, 0.0)
    query_part, key_part, value_part = ring_project(picked, (w_query, w_key, w_value), "tp")
    queries = (
        rotate(query_part.reshape(slot_count, heads_local, head_dim), position) * head_dim ** (-0.5)
    ).astype(jnp.bfloat16)
    key_rows = rotate(key_part.reshape(slot_count, kv_local, head_dim), position).astype(
        jnp.bfloat16
    )
    value_rows = value_part.reshape(slot_count, kv_local, head_dim).astype(jnp.bfloat16)
    payload = pack_payload(key_rows, value_rows, chosen)
    payload = lax.all_gather(payload, "ctx", axis=0, tiled=True)
    blocks = payload.reshape(shards, slot_count + EXTRA_ROWS, 2 * kv_width)
    chosen_all = unpack_chosen(blocks, slot_count, kv_width)
    shard_base = (jnp.arange(shards, dtype=jnp.int32) * seq_rows)[:, None]
    key_pos = jnp.where(chosen_all < seq_rows, shard_base + chosen_all, pad_mark)
    counts = jnp.sum((chosen_all < seq_rows).astype(jnp.int32), axis=1)
    q_blocks = (jnp.sum(live.astype(jnp.int32)) + (SUB - 1)) // SUB
    scalars = jnp.concatenate(
        [jnp.stack([lax.axis_index("ctx"), q_blocks]).astype(jnp.int32), counts]
    )
    q_tiles = slot_count // SUB
    flat_q = jnp.transpose(
        queries.reshape(q_tiles, SUB, group, head_dim), (0, 2, 1, 3)
    ).reshape(slot_count * group, head_dim)

    def per_row(values):
        spread = jnp.broadcast_to(values.reshape(q_tiles, 1, SUB), (q_tiles, group, SUB))
        return spread.reshape(slot_count * group, 1)

    out = attend(
        scalars, flat_q, per_row(position), per_row(gated), blocks, key_pos.reshape(shards, 1, slot_count)
    )
    out = jnp.transpose(out.reshape(q_tiles, group, SUB, head_dim), (0, 2, 1, 3))
    return out.reshape(slot_count, query_width)


def solution(mesh):
    placed = (P("ctx", "tp"), P("ctx"), P("ctx"), P(None, "tp"), P(None, "tp"), P(None, "tp"))
    return jax.shard_map(
        body, mesh=mesh, in_specs=placed, out_specs=P("ctx", "tp"), check_vma=False
    )
```

```python
import functools
import math

import jax
import jax.numpy as jnp
from jax import lax
from jax.experimental import pallas as pl
from jax.experimental.pallas import tpu as pltpu
from jax.sharding import PartitionSpec as P

HEAD_DIM = 128


ROPE_BASE = 500000.0
MASKED = -1e30
SUB = 128


def rotate(values_in, position):
    half_dim = values_in.shape[-1] // 2
    frequency = jnp.exp(
        jnp.arange(half_dim, dtype=jnp.float32) * (-2.0 * math.log(ROPE_BASE) / values_in.shape[-1])
    )
    angles = position.astype(jnp.float32)[:, None] * frequency[None, :]
    cosine = jnp.cos(angles)[:, None, :]
    sine = jnp.sin(angles)[:, None, :]
    first = values_in[..., :half_dim]
    second = values_in[..., half_dim:]
    return jnp.concatenate(
        [first * cosine - second * sine, second * cosine + first * sine], axis=-1
    )


def attend_kernel(scalars, q_ref, qpos_ref, kpos_ref, gate_ref, kv_ref, out_ref, m_scr, l_scr, acc_scr, *, cols, shards):
    t = pl.program_id(0)
    own = scalars[0]
    q_blocks = scalars[1]
    count = scalars[2 + t]
    key_blocks = (count + (SUB - 1)) // SUB
    head_dim = q_ref.shape[0]
    pieces = kv_ref.shape[1] // SUB

    @pl.when(t == 0)
    def _():
        m_scr[...] = jnp.full(m_scr.shape, MASKED, jnp.float32)
        l_scr[...] = jnp.zeros(l_scr.shape, jnp.float32)
        acc_scr[...] = jnp.zeros(acc_scr.shape, jnp.float32)

    def step(qb, width, diagonal):
        c0 = qb * cols
        q = q_ref[:, c0:c0 + cols]
        scores = jnp.concatenate(
            [
                jnp.dot(kv_ref[0:SUB, j * SUB:(j + 1) * SUB], q, preferred_element_type=jnp.float32)
                for j in range(width // SUB)
            ],
            axis=0,
        )
        if diagonal:
            allowed = kpos_ref[0:width, :] <= qpos_ref[:, c0:c0 + cols]
        else:
            allowed = lax.broadcasted_iota(jnp.int32, scores.shape, 0) < count
        m_prev = m_scr[:, c0:c0 + cols]
        m_new = jnp.maximum(m_prev, jnp.max(jnp.where(allowed, scores, MASKED), axis=0, keepdims=True))
        alpha = jnp.exp(m_prev - m_new)
        p = jnp.where(allowed, jnp.exp(scores - m_new), 0.0)
        l_scr[:, c0:c0 + cols] = alpha * l_scr[:, c0:c0 + cols] + jnp.sum(p, axis=0, keepdims=True)
        acc_scr[:, c0:c0 + cols] = alpha * acc_scr[:, c0:c0 + cols] + jnp.dot(
            kv_ref[SUB:SUB + head_dim, 0:width], p.astype(jnp.bfloat16), preferred_element_type=jnp.float32
        )
        m_scr[:, c0:c0 + cols] = m_new

    for qb in range(q_ref.shape[1] // cols):
        for blocks in range(1, pieces + 1):
            for diagonal in (False, True):
                hit = (t == own) if diagonal else (t < own)

                @pl.when(hit & (qb < q_blocks) & (key_blocks == blocks))
                def _():
                    step(qb, blocks * SUB, diagonal)

    @pl.when(t == shards - 1)
    def _():
        total = l_scr[...]
        denom = jnp.where(total > 0.0, total, 1.0)
        out_ref[...] = ((acc_scr[...] / denom) * gate_ref[...]).astype(out_ref.dtype)


def attend(scalars, q, qpos, kpos, gate, kv, interpret=False):
    head_dim, q_rows = q.shape
    shards, kv_rows, slots = kv.shape
    cols = kpos.shape[1]
    kernel = functools.partial(attend_kernel, cols=cols, shards=shards)

    def fixed(t, sc):
        return (0, 0)

    grid_spec = pltpu.PrefetchScalarGridSpec(
        num_scalar_prefetch=1,
        grid=(shards,),
        in_specs=[
            pl.BlockSpec((head_dim, q_rows), fixed),
            pl.BlockSpec((1, q_rows), fixed),
            pl.BlockSpec((slots, cols), fixed),
            pl.BlockSpec((1, q_rows), fixed),
            pl.BlockSpec((None, SUB + head_dim, slots), lambda t, sc: (jnp.minimum(t, sc[0]), 0, 0)),
        ],
        out_specs=pl.BlockSpec((head_dim, q_rows), fixed),
        scratch_shapes=[
            pltpu.VMEM((1, q_rows), jnp.float32),
            pltpu.VMEM((1, q_rows), jnp.float32),
            pltpu.VMEM((head_dim, q_rows), jnp.float32),
        ],
    )
    return pl.pallas_call(
        kernel,
        grid_spec=grid_spec,
        out_shape=jax.ShapeDtypeStruct((head_dim, q_rows), jnp.bfloat16),
        compiler_params=pltpu.CompilerParams(dimension_semantics=("arbitrary",)),
        interpret=interpret,
    )(scalars, q, qpos, kpos, gate, kv)


FLAG_ROWS = 16


def pack_payload(key_rows, value_rows, live):
    slot_count = live.shape[0]
    head_dim = key_rows.shape[-1]
    keys = key_rows.reshape(slot_count // SUB, SUB, head_dim)
    keys = jnp.transpose(keys, (1, 0, 2)).reshape(SUB, slot_count)
    values = jnp.transpose(value_rows.reshape(slot_count, head_dim))
    flags = jnp.zeros((FLAG_ROWS, slot_count), jnp.bfloat16).at[0].set(live.astype(jnp.bfloat16))
    return jnp.concatenate([keys, values, flags], axis=0)


def ring_project(picked, weights, axis):
    size = lax.axis_size(axis)
    idx = lax.axis_index(axis)
    width = picked.shape[1]
    forward = [(i, (i + 1) % size) for i in range(size)]
    backward = [(i, (i - 1) % size) for i in range(size)]

    def partial(block, source):
        start = source * width
        return [
            jnp.dot(block, lax.dynamic_slice_in_dim(w, start, width, axis=0), preferred_element_type=jnp.float32)
            for w in weights
        ]

    sums = partial(picked, idx)
    ahead = picked
    behind = picked
    steps_ahead = size // 2
    steps_behind = size - 1 - steps_ahead
    for step in range(1, steps_ahead + 1):
        ahead = lax.ppermute(ahead, axis, forward)
        parts = [partial(ahead, (idx - step) % size)]
        if step <= steps_behind:
            behind = lax.ppermute(behind, axis, backward)
            parts.append(partial(behind, (idx + step) % size))
        for part in parts:
            sums = [s + p for s, p in zip(sums, part)]
    return sums


def body(hidden_states, chosen, router_gate, w_query, w_key, w_value):
    seq_rows = hidden_states.shape[0]
    slot_count = chosen.shape[0]
    head_dim = HEAD_DIM
    query_width = w_query.shape[1]
    kv_width = w_key.shape[1]
    kv_local = kv_width // head_dim
    heads_local = query_width // head_dim
    group = heads_local // kv_local
    shards = lax.axis_size("ctx")
    live = chosen < seq_rows
    pad_mark = shards * seq_rows + 1
    position = jnp.where(live, lax.axis_index("ctx") * seq_rows + chosen, pad_mark)
    picked = hidden_states[jnp.minimum(chosen, seq_rows - 1)]
    gated = jnp.where(live, router_gate, 0.0)
    query_part, key_part, value_part = ring_project(picked, (w_query, w_key, w_value), "tp")
    queries = (
        rotate(query_part.reshape(slot_count, heads_local, head_dim), position) * head_dim ** (-0.5)
    ).astype(jnp.bfloat16)
    key_rows = rotate(key_part.reshape(slot_count, kv_local, head_dim), position).astype(
        jnp.bfloat16
    )
    value_rows = value_part.reshape(slot_count, kv_local, head_dim).astype(jnp.bfloat16)
    payload = pack_payload(key_rows, value_rows, live)
    payload = lax.all_gather(payload, "ctx", axis=0, tiled=True)
    blocks = payload.reshape(shards, payload.shape[0] // shards, slot_count)
    flag_row = blocks.shape[1] - FLAG_ROWS
    counts = jnp.sum(blocks[:, flag_row, :].astype(jnp.float32), axis=1).astype(jnp.int32)
    q_blocks = (jnp.sum(live.astype(jnp.int32)) + (SUB - 1)) // SUB
    scalars = jnp.concatenate(
        [jnp.stack([lax.axis_index("ctx"), q_blocks]).astype(jnp.int32), counts]
    )
    q_tiles = slot_count // SUB
    flat_q = jnp.transpose(
        queries.reshape(q_tiles, SUB, group, head_dim), (0, 2, 1, 3)
    ).reshape(slot_count * group, head_dim)

    def per_column(values):
        spread = jnp.broadcast_to(values.reshape(q_tiles, 1, SUB), (q_tiles, group, SUB))
        return spread.reshape(1, slot_count * group)

    own_pos = jnp.broadcast_to(chosen[:, None], (slot_count, group * SUB))
    out = attend(
        scalars, jnp.transpose(flat_q), per_column(chosen), own_pos, per_column(gated), blocks
    )
    out = jnp.transpose(jnp.transpose(out).reshape(q_tiles, group, SUB, head_dim), (0, 2, 1, 3))
    return out.reshape(slot_count, query_width)


def solution(mesh):
    placed = (P("ctx", "tp"), P("ctx"), P("ctx"), P(None, "tp"), P(None, "tp"), P(None, "tp"))
    return jax.shard_map(
        body, mesh=mesh, in_specs=placed, out_specs=P("ctx", "tp"), check_vma=False
    )
```

```python
import functools
import math

import jax
import jax.numpy as jnp
from jax import lax
from jax.experimental import pallas as pl
from jax.experimental.pallas import tpu as pltpu
from jax.sharding import PartitionSpec as P

HEAD_DIM = 128


ROPE_BASE = 500000.0
MASKED = -1e30
SUB = 128


def rotate(values_in, position):
    half_dim = values_in.shape[-1] // 2
    frequency = jnp.exp(
        jnp.arange(half_dim, dtype=jnp.float32) * (-2.0 * math.log(ROPE_BASE) / values_in.shape[-1])
    )
    angles = position.astype(jnp.float32)[:, None] * frequency[None, :]
    cosine = jnp.cos(angles)[:, None, :]
    sine = jnp.sin(angles)[:, None, :]
    first = values_in[..., :half_dim]
    second = values_in[..., half_dim:]
    return jnp.concatenate(
        [first * cosine - second * sine, second * cosine + first * sine], axis=-1
    )


def attend_kernel(scalars, q_ref, qpos_ref, kpos_ref, kv_ref, acc_ref, m_ref, l_ref, *, cols, steps):
    i = pl.program_id(0)
    first = scalars[0]
    active = i < scalars[1]
    q_blocks = scalars[2]
    diagonal_shard = scalars[3]
    t = first + i
    count = scalars[4 + jnp.minimum(t, scalars.shape[0] - 5)]
    key_blocks = (count + (SUB - 1)) // SUB
    head_dim = q_ref.shape[0]
    pieces = kv_ref.shape[1] // SUB

    @pl.when(i == 0)
    def _():
        m_ref[...] = jnp.full(m_ref.shape, MASKED, jnp.float32)
        l_ref[...] = jnp.zeros(l_ref.shape, jnp.float32)
        acc_ref[...] = jnp.zeros(acc_ref.shape, jnp.float32)

    def step(qb, width, diagonal):
        c0 = qb * cols
        q = q_ref[:, c0:c0 + cols]
        scores = jnp.concatenate(
            [
                jnp.dot(kv_ref[0:SUB, j * SUB:(j + 1) * SUB], q, preferred_element_type=jnp.float32)
                for j in range(width // SUB)
            ],
            axis=0,
        )
        if diagonal:
            allowed = kpos_ref[0:width, :] <= qpos_ref[:, c0:c0 + cols]
        else:
            allowed = lax.broadcasted_iota(jnp.int32, scores.shape, 0) < count
        m_prev = m_ref[:, c0:c0 + cols]
        m_new = jnp.maximum(m_prev, jnp.max(jnp.where(allowed, scores, MASKED), axis=0, keepdims=True))
        alpha = jnp.exp(m_prev - m_new)
        p = jnp.where(allowed, jnp.exp(scores - m_new), 0.0)
        l_ref[:, c0:c0 + cols] = alpha * l_ref[:, c0:c0 + cols] + jnp.sum(p, axis=0, keepdims=True)
        acc_ref[:, c0:c0 + cols] = alpha * acc_ref[:, c0:c0 + cols] + jnp.dot(
            kv_ref[SUB:SUB + head_dim, 0:width], p.astype(jnp.bfloat16), preferred_element_type=jnp.float32
        )
        m_ref[:, c0:c0 + cols] = m_new

    for qb in range(q_ref.shape[1] // cols):
        for blocks in range(1, pieces + 1):
            for diagonal in (False, True):
                hit = (t == diagonal_shard) if diagonal else (t != diagonal_shard)

                @pl.when(active & hit & (qb < q_blocks) & (key_blocks == blocks))
                def _():
                    step(qb, blocks * SUB, diagonal)


def attend(scalars, q, qpos, kpos, kv, steps, interpret=False):
    head_dim, q_rows = q.shape
    shards, kv_rows, slots = kv.shape
    cols = kpos.shape[1]
    kernel = functools.partial(attend_kernel, cols=cols, steps=steps)

    def fixed(i, sc):
        return (0, 0)

    def shard_of(i, sc):
        last = jnp.maximum(sc[1] - 1, 0)
        return (jnp.clip(sc[0] + jnp.minimum(i, last), 0, shards - 1), 0, 0)

    grid_spec = pltpu.PrefetchScalarGridSpec(
        num_scalar_prefetch=1,
        grid=(steps,),
        in_specs=[
            pl.BlockSpec((head_dim, q_rows), fixed),
            pl.BlockSpec((1, q_rows), fixed),
            pl.BlockSpec((slots, cols), fixed),
            pl.BlockSpec((None, SUB + head_dim, slots), shard_of),
        ],
        out_specs=[
            pl.BlockSpec((head_dim, q_rows), fixed),
            pl.BlockSpec((1, q_rows), fixed),
            pl.BlockSpec((1, q_rows), fixed),
        ],
    )
    return pl.pallas_call(
        kernel,
        grid_spec=grid_spec,
        out_shape=[
            jax.ShapeDtypeStruct((head_dim, q_rows), jnp.float32),
            jax.ShapeDtypeStruct((1, q_rows), jnp.float32),
            jax.ShapeDtypeStruct((1, q_rows), jnp.float32),
        ],
        compiler_params=pltpu.CompilerParams(dimension_semantics=("arbitrary",)),
        interpret=interpret,
    )(scalars, q, qpos, kpos, kv)


def merge(first, second):
    acc_a, m_a, l_a = first
    acc_b, m_b, l_b = second
    m_a = jnp.where(l_a > 0.0, m_a, MASKED)
    m_b = jnp.where(l_b > 0.0, m_b, MASKED)
    m = jnp.maximum(m_a, m_b)
    scale_a = jnp.exp(m_a - m)
    scale_b = jnp.exp(m_b - m)
    return acc_a * scale_a + acc_b * scale_b, l_a * scale_a + l_b * scale_b


FLAG_ROWS = 16


def pack_payload(key_rows, value_rows, live):
    slot_count = live.shape[0]
    head_dim = key_rows.shape[-1]
    keys = key_rows.reshape(slot_count // SUB, SUB, head_dim)
    keys = jnp.transpose(keys, (1, 0, 2)).reshape(SUB, slot_count)
    values = jnp.transpose(value_rows.reshape(slot_count, head_dim))
    flags = jnp.zeros((FLAG_ROWS, slot_count), jnp.bfloat16).at[0].set(live.astype(jnp.bfloat16))
    return jnp.concatenate([keys, values, flags], axis=0)


def ring_project(picked, weights, axis):
    size = lax.axis_size(axis)
    idx = lax.axis_index(axis)
    width = picked.shape[1]
    forward = [(i, (i + 1) % size) for i in range(size)]
    backward = [(i, (i - 1) % size) for i in range(size)]

    def partial(block, source):
        start = source * width
        return [
            jnp.dot(block, lax.dynamic_slice_in_dim(w, start, width, axis=0), preferred_element_type=jnp.float32)
            for w in weights
        ]

    sums = partial(picked, idx)
    ahead = picked
    behind = picked
    steps_ahead = size // 2
    steps_behind = size - 1 - steps_ahead
    for step in range(1, steps_ahead + 1):
        ahead = lax.ppermute(ahead, axis, forward)
        parts = [partial(ahead, (idx - step) % size)]
        if step <= steps_behind:
            behind = lax.ppermute(behind, axis, backward)
            parts.append(partial(behind, (idx + step) % size))
        for part in parts:
            sums = [s + p for s, p in zip(sums, part)]
    return sums


def body(hidden_states, chosen, router_gate, w_query, w_key, w_value):
    seq_rows = hidden_states.shape[0]
    slot_count = chosen.shape[0]
    head_dim = HEAD_DIM
    query_width = w_query.shape[1]
    kv_width = w_key.shape[1]
    kv_local = kv_width // head_dim
    heads_local = query_width // head_dim
    group = heads_local // kv_local
    shards = lax.axis_size("ctx")
    live = chosen < seq_rows
    pad_mark = shards * seq_rows + 1
    position = jnp.where(live, lax.axis_index("ctx") * seq_rows + chosen, pad_mark)
    picked = hidden_states[jnp.minimum(chosen, seq_rows - 1)]
    gated = jnp.where(live, router_gate, 0.0)
    query_part, key_part, value_part = ring_project(picked, (w_query, w_key, w_value), "tp")
    queries = (
        rotate(query_part.reshape(slot_count, heads_local, head_dim), position) * head_dim ** (-0.5)
    ).astype(jnp.bfloat16)
    key_rows = rotate(key_part.reshape(slot_count, kv_local, head_dim), position).astype(
        jnp.bfloat16
    )
    value_rows = value_part.reshape(slot_count, kv_local, head_dim).astype(jnp.bfloat16)
    payload = pack_payload(key_rows, value_rows, live)
    payload = lax.all_gather(payload, "ctx", axis=0, tiled=True)
    blocks = payload.reshape(shards, payload.shape[0] // shards, slot_count)
    flag_row = blocks.shape[1] - FLAG_ROWS
    counts = jnp.sum(blocks[:, flag_row, :].astype(jnp.float32), axis=1).astype(jnp.int32)
    own = lax.axis_index("ctx")
    half = shards // 2
    partner = shards - 1 - own

    def live_blocks(count):
        return (count + (SUB - 1)) // SUB

    def scalars_of(first, count, q_blocks, diagonal):
        head = jnp.stack([first, count, q_blocks, diagonal]).astype(jnp.int32)
        return jnp.concatenate([head, counts])

    q_tiles = slot_count // SUB
    flat_q = jnp.transpose(
        queries.reshape(q_tiles, SUB, group, head_dim), (0, 2, 1, 3)
    ).reshape(slot_count * group, head_dim)
    own_q = jnp.transpose(flat_q)

    def per_column(values):
        spread = jnp.broadcast_to(values.reshape(q_tiles, 1, SUB), (q_tiles, group, SUB))
        return spread.reshape(1, slot_count * group)

    own_pos = jnp.broadcast_to(chosen[:, None], (slot_count, group * SUB))
    query_pos = per_column(chosen)
    guest_q = lax.ppermute(own_q, "ctx", [(j, shards - 1 - j) for j in range(half, shards)])
    guest_count = jnp.maximum(half - own, 0)
    guest_scalars = scalars_of(
        jnp.int32(0), guest_count, live_blocks(counts[partner]), jnp.int32(-1)
    )

    def guest_work(q):
        return tuple(attend(guest_scalars, q, query_pos, own_pos, blocks, half))

    def no_guest(q):
        rows = (1, q.shape[1])
        return (
            jnp.zeros(q.shape, jnp.float32),
            jnp.full(rows, MASKED, jnp.float32),
            jnp.zeros(rows, jnp.float32),
        )

    guest_state = lax.cond(guest_count > 0, guest_work, no_guest, guest_q)
    returned = lax.ppermute(guest_state, "ctx", [(j, shards - 1 - j) for j in range(half)])
    own_q, guest_state = lax.optimization_barrier((own_q, guest_state))
    own_first = jnp.maximum(own - (half - 1), 0)
    own_scalars = scalars_of(
        own_first, own - own_first + 1, live_blocks(jnp.sum(live.astype(jnp.int32))), own
    )
    own_state = tuple(attend(own_scalars, own_q, query_pos, own_pos, blocks, half))
    acc, total = merge(own_state, returned)
    out = (acc / jnp.where(total > 0.0, total, 1.0)) * per_column(gated)
    out = jnp.transpose(out.astype(jnp.bfloat16))
    out = jnp.transpose(out.reshape(q_tiles, group, SUB, head_dim), (0, 2, 1, 3))
    return out.reshape(slot_count, query_width)


def solution(mesh):
    placed = (P("ctx", "tp"), P("ctx"), P("ctx"), P(None, "tp"), P(None, "tp"), P(None, "tp"))
    return jax.shard_map(
        body, mesh=mesh, in_specs=placed, out_specs=P("ctx", "tp"), check_vma=False
    )
```

```python
import functools
import math

import jax
import jax.numpy as jnp
from jax import lax
from jax.experimental import pallas as pl
from jax.experimental.pallas import tpu as pltpu
from jax.sharding import PartitionSpec as P

HEAD_DIM = 128


ROPE_BASE = 500000.0
MASKED = -1e30
SUB = 128


def rotate(values_in, position):
    half_dim = values_in.shape[-1] // 2
    frequency = jnp.exp(
        jnp.arange(half_dim, dtype=jnp.float32) * (-2.0 * math.log(ROPE_BASE) / values_in.shape[-1])
    )
    angles = position.astype(jnp.float32)[:, None] * frequency[None, :]
    cosine = jnp.cos(angles)[:, None, :]
    sine = jnp.sin(angles)[:, None, :]
    first = values_in[..., :half_dim]
    second = values_in[..., half_dim:]
    return jnp.concatenate(
        [first * cosine - second * sine, second * cosine + first * sine], axis=-1
    )


def attend_kernel(scalars, q_ref, qpos_ref, kpos_ref, kv_ref, acc_ref, m_ref, l_ref, *, cols, steps):
    i = pl.program_id(0)
    first = scalars[0]
    active = i < scalars[1]
    q_blocks = scalars[2]
    diagonal_shard = scalars[3]
    t = first + i
    count = scalars[4 + jnp.minimum(t, scalars.shape[0] - 5)]
    key_blocks = (count + (SUB - 1)) // SUB
    head_dim = q_ref.shape[0]
    pieces = kv_ref.shape[1] // SUB

    @pl.when(i == 0)
    def _():
        m_ref[...] = jnp.full(m_ref.shape, MASKED, jnp.float32)
        l_ref[...] = jnp.zeros(l_ref.shape, jnp.float32)
        acc_ref[...] = jnp.zeros(acc_ref.shape, jnp.float32)

    def step(qb, width, diagonal):
        c0 = qb * cols
        q = q_ref[:, c0:c0 + cols]
        chunks = [
            jnp.dot(kv_ref[0:SUB, j * SUB:(j + 1) * SUB], q, preferred_element_type=jnp.float32)
            for j in range(width // SUB)
        ]
        if diagonal:
            masks = [kpos_ref[j * SUB:(j + 1) * SUB, :] <= qpos_ref[:, c0:c0 + cols] for j in range(len(chunks))]
        else:
            last = lax.broadcasted_iota(jnp.int32, chunks[-1].shape, 0) + (width - SUB) < count
            masks = [None] * (len(chunks) - 1) + [last]
        m_prev = m_ref[:, c0:c0 + cols]
        m_new = m_prev
        for chunk, mask in zip(chunks, masks):
            kept = chunk if mask is None else jnp.where(mask, chunk, MASKED)
            m_new = jnp.maximum(m_new, jnp.max(kept, axis=0, keepdims=True))
        alpha = jnp.exp(m_prev - m_new)
        weights = []
        for chunk, mask in zip(chunks, masks):
            w = jnp.exp(chunk - m_new)
            weights.append(w if mask is None else jnp.where(mask, w, 0.0))
        p = jnp.concatenate(weights, axis=0)
        l_ref[:, c0:c0 + cols] = alpha * l_ref[:, c0:c0 + cols] + jnp.sum(p, axis=0, keepdims=True)
        acc_ref[:, c0:c0 + cols] = alpha * acc_ref[:, c0:c0 + cols] + jnp.dot(
            kv_ref[SUB:SUB + head_dim, 0:width], p.astype(jnp.bfloat16), preferred_element_type=jnp.float32
        )
        m_ref[:, c0:c0 + cols] = m_new

    for qb in range(q_ref.shape[1] // cols):
        for blocks in range(1, pieces + 1):
            for diagonal in (False, True):
                hit = (t == diagonal_shard) if diagonal else (t != diagonal_shard)

                @pl.when(active & hit & (qb < q_blocks) & (key_blocks == blocks))
                def _():
                    step(qb, blocks * SUB, diagonal)


def attend(scalars, q, qpos, kpos, kv, steps, interpret=False):
    head_dim, q_rows = q.shape
    shards, kv_rows, slots = kv.shape
    cols = kpos.shape[1]
    kernel = functools.partial(attend_kernel, cols=cols, steps=steps)

    def fixed(i, sc):
        return (0, 0)

    def shard_of(i, sc):
        last = jnp.maximum(sc[1] - 1, 0)
        return (jnp.clip(sc[0] + jnp.minimum(i, last), 0, shards - 1), 0, 0)

    grid_spec = pltpu.PrefetchScalarGridSpec(
        num_scalar_prefetch=1,
        grid=(steps,),
        in_specs=[
            pl.BlockSpec((head_dim, q_rows), fixed),
            pl.BlockSpec((1, q_rows), fixed),
            pl.BlockSpec((slots, cols), fixed),
            pl.BlockSpec((None, SUB + head_dim, slots), shard_of),
        ],
        out_specs=[
            pl.BlockSpec((head_dim, q_rows), fixed),
            pl.BlockSpec((1, q_rows), fixed),
            pl.BlockSpec((1, q_rows), fixed),
        ],
    )
    return pl.pallas_call(
        kernel,
        grid_spec=grid_spec,
        out_shape=[
            jax.ShapeDtypeStruct((head_dim, q_rows), jnp.float32),
            jax.ShapeDtypeStruct((1, q_rows), jnp.float32),
            jax.ShapeDtypeStruct((1, q_rows), jnp.float32),
        ],
        compiler_params=pltpu.CompilerParams(dimension_semantics=("arbitrary",)),
        interpret=interpret,
    )(scalars, q, qpos, kpos, kv)


def merge(first, second):
    acc_a, m_a, l_a = first
    acc_b, m_b, l_b = second
    m_a = jnp.where(l_a > 0.0, m_a, MASKED)
    m_b = jnp.where(l_b > 0.0, m_b, MASKED)
    m = jnp.maximum(m_a, m_b)
    scale_a = jnp.exp(m_a - m)
    scale_b = jnp.exp(m_b - m)
    return acc_a * scale_a + acc_b * scale_b, l_a * scale_a + l_b * scale_b


FLAG_ROWS = 16
EXTRA_OWN = 1


def pack_payload(key_rows, value_rows, live):
    slot_count = live.shape[0]
    head_dim = key_rows.shape[-1]
    keys = key_rows.reshape(slot_count // SUB, SUB, head_dim)
    keys = jnp.transpose(keys, (1, 0, 2)).reshape(SUB, slot_count)
    values = jnp.transpose(value_rows.reshape(slot_count, head_dim))
    flags = jnp.zeros((FLAG_ROWS, slot_count), jnp.bfloat16).at[0].set(live.astype(jnp.bfloat16))
    return jnp.concatenate([keys, values, flags], axis=0)


def ring_project(picked, weights, axis):
    size = lax.axis_size(axis)
    idx = lax.axis_index(axis)
    width = picked.shape[1]
    forward = [(i, (i + 1) % size) for i in range(size)]
    backward = [(i, (i - 1) % size) for i in range(size)]

    def partial(block, source):
        start = source * width
        return [
            jnp.dot(block, lax.dynamic_slice_in_dim(w, start, width, axis=0), preferred_element_type=jnp.float32)
            for w in weights
        ]

    sums = partial(picked, idx)
    ahead = picked
    behind = picked
    steps_behind = (size - 1) // 2
    for step in range(1, steps_behind + 1):
        ahead = lax.ppermute(ahead, axis, forward)
        behind = lax.ppermute(behind, axis, backward)
        for part in (partial(ahead, (idx - step) % size), partial(behind, (idx + step) % size)):
            sums = [s + p for s, p in zip(sums, part)]
    if size % 2 == 0:
        rows = picked.shape[0] // 2
        top = lax.ppermute(ahead[:rows], axis, forward)
        bottom = lax.ppermute(behind[rows:], axis, backward)
        part = partial(jnp.concatenate([top, bottom], axis=0), (idx + size // 2) % size)
        sums = [s + p for s, p in zip(sums, part)]
    return sums


def body(hidden_states, chosen, router_gate, w_query, w_key, w_value):
    seq_rows = hidden_states.shape[0]
    slot_count = chosen.shape[0]
    head_dim = HEAD_DIM
    query_width = w_query.shape[1]
    kv_width = w_key.shape[1]
    kv_local = kv_width // head_dim
    heads_local = query_width // head_dim
    group = heads_local // kv_local
    shards = lax.axis_size("ctx")
    live = chosen < seq_rows
    pad_mark = shards * seq_rows + 1
    position = jnp.where(live, lax.axis_index("ctx") * seq_rows + chosen, pad_mark)
    picked = hidden_states[jnp.minimum(chosen, seq_rows - 1)]
    gated = jnp.where(live, router_gate, 0.0)
    query_part, key_part, value_part = ring_project(picked, (w_query, w_key, w_value), "tp")
    queries = (
        rotate(query_part.reshape(slot_count, heads_local, head_dim), position) * head_dim ** (-0.5)
    ).astype(jnp.bfloat16)
    key_rows = rotate(key_part.reshape(slot_count, kv_local, head_dim), position).astype(
        jnp.bfloat16
    )
    value_rows = value_part.reshape(slot_count, kv_local, head_dim).astype(jnp.bfloat16)
    payload = pack_payload(key_rows, value_rows, live)
    payload = lax.all_gather(payload, "ctx", axis=0, tiled=True)
    blocks = payload.reshape(shards, payload.shape[0] // shards, slot_count)
    flag_row = blocks.shape[1] - FLAG_ROWS
    counts = jnp.sum(blocks[:, flag_row, :].astype(jnp.float32), axis=1).astype(jnp.int32)
    own = lax.axis_index("ctx")
    half = shards // 2
    partner = shards - 1 - own

    def live_blocks(count):
        return (count + (SUB - 1)) // SUB

    def scalars_of(first, count, q_blocks, diagonal):
        head = jnp.stack([first, count, q_blocks, diagonal]).astype(jnp.int32)
        return jnp.concatenate([head, counts])

    q_tiles = slot_count // SUB
    flat_q = jnp.transpose(
        queries.reshape(q_tiles, SUB, group, head_dim), (0, 2, 1, 3)
    ).reshape(slot_count * group, head_dim)
    own_q = jnp.transpose(flat_q)

    def per_column(values):
        spread = jnp.broadcast_to(values.reshape(q_tiles, 1, SUB), (q_tiles, group, SUB))
        return spread.reshape(1, slot_count * group)

    own_pos = jnp.broadcast_to(chosen[:, None], (slot_count, group * SUB))
    query_pos = per_column(chosen)
    guest_q = lax.ppermute(own_q, "ctx", [(j, shards - 1 - j) for j in range(half, shards)])
    guest_count = jnp.maximum(half - EXTRA_OWN - own, 0)
    guest_scalars = scalars_of(
        jnp.int32(0), guest_count, live_blocks(counts[partner]), jnp.int32(-1)
    )

    def guest_work(q):
        return tuple(attend(guest_scalars, q, query_pos, own_pos, blocks, half - EXTRA_OWN))

    def no_guest(q):
        rows = (1, q.shape[1])
        return (
            jnp.zeros(q.shape, jnp.float32),
            jnp.full(rows, MASKED, jnp.float32),
            jnp.zeros(rows, jnp.float32),
        )

    guest_state = lax.cond(guest_count > 0, guest_work, no_guest, guest_q)
    returned = lax.ppermute(guest_state, "ctx", [(j, shards - 1 - j) for j in range(half)])
    own_q, guest_state = lax.optimization_barrier((own_q, guest_state))
    own_first = jnp.maximum(own - (half - 1) - EXTRA_OWN, 0)
    own_scalars = scalars_of(
        own_first, own - own_first + 1, live_blocks(jnp.sum(live.astype(jnp.int32))), own
    )
    own_state = tuple(attend(own_scalars, own_q, query_pos, own_pos, blocks, half + EXTRA_OWN))
    acc, total = merge(own_state, returned)
    out = (acc / jnp.where(total > 0.0, total, 1.0)) * per_column(gated)
    out = jnp.transpose(out.astype(jnp.bfloat16))
    out = jnp.transpose(out.reshape(q_tiles, group, SUB, head_dim), (0, 2, 1, 3))
    return out.reshape(slot_count, query_width)


def solution(mesh):
    placed = (P("ctx", "tp"), P("ctx"), P("ctx"), P(None, "tp"), P(None, "tp"), P(None, "tp"))
    return jax.shard_map(
        body, mesh=mesh, in_specs=placed, out_specs=P("ctx", "tp"), check_vma=False
    )
```

```python
import functools
import math

import jax
import jax.numpy as jnp
from jax import lax
from jax.experimental import pallas as pl
from jax.experimental.pallas import tpu as pltpu
from jax.sharding import PartitionSpec as P

HEAD_DIM = 128


ROPE_BASE = 500000.0
MASKED = -1e30
SUB = 128
STATE_ROWS = 8


def rotate(values_in, position):
    half_dim = values_in.shape[-1] // 2
    frequency = jnp.exp(
        jnp.arange(half_dim, dtype=jnp.float32) * (-2.0 * math.log(ROPE_BASE) / values_in.shape[-1])
    )
    angles = position.astype(jnp.float32)[:, None] * frequency[None, :]
    cosine = jnp.cos(angles)[:, None, :]
    sine = jnp.sin(angles)[:, None, :]
    first = values_in[..., :half_dim]
    second = values_in[..., half_dim:]
    return jnp.concatenate(
        [first * cosine - second * sine, second * cosine + first * sine], axis=-1
    )


def attend_kernel(scalars, q_ref, qpos_ref, kpos_ref, kv_ref, state_ref, *, cols, steps):
    i = pl.program_id(0)
    first = scalars[0]
    active = i < scalars[1]
    q_blocks = scalars[2]
    diagonal_shard = scalars[3]
    t = first + i
    count = scalars[4 + jnp.minimum(t, scalars.shape[0] - 5)]
    key_blocks = (count + (SUB - 1)) // SUB
    head_dim = q_ref.shape[0]
    pieces = kv_ref.shape[1] // SUB

    acc_ref = state_ref.at[0:head_dim, :]
    m_ref = state_ref.at[head_dim:head_dim + 1, :]
    l_ref = state_ref.at[head_dim + 1:head_dim + 2, :]

    @pl.when(i == 0)
    def _():
        state_ref[...] = jnp.zeros(state_ref.shape, jnp.float32)
        m_ref[...] = jnp.full(m_ref.shape, MASKED, jnp.float32)

    def step(qb, width, diagonal):
        c0 = qb * cols
        q = q_ref[:, c0:c0 + cols]
        chunks = [
            jnp.dot(kv_ref[0:SUB, j * SUB:(j + 1) * SUB], q, preferred_element_type=jnp.float32)
            for j in range(width // SUB)
        ]
        if diagonal:
            masks = [kpos_ref[j * SUB:(j + 1) * SUB, :] <= qpos_ref[:, c0:c0 + cols] for j in range(len(chunks))]
        else:
            last = lax.broadcasted_iota(jnp.int32, chunks[-1].shape, 0) + (width - SUB) < count
            masks = [None] * (len(chunks) - 1) + [last]
        m_prev = m_ref[:, c0:c0 + cols]
        m_new = m_prev
        for chunk, mask in zip(chunks, masks):
            kept = chunk if mask is None else jnp.where(mask, chunk, MASKED)
            m_new = jnp.maximum(m_new, jnp.max(kept, axis=0, keepdims=True))
        alpha = jnp.exp(m_prev - m_new)
        weights = []
        for chunk, mask in zip(chunks, masks):
            w = jnp.exp(chunk - m_new)
            weights.append(w if mask is None else jnp.where(mask, w, 0.0))
        p = jnp.concatenate(weights, axis=0)
        l_ref[:, c0:c0 + cols] = alpha * l_ref[:, c0:c0 + cols] + jnp.sum(p, axis=0, keepdims=True)
        acc_ref[:, c0:c0 + cols] = alpha * acc_ref[:, c0:c0 + cols] + jnp.dot(
            kv_ref[SUB:SUB + head_dim, 0:width], p.astype(jnp.bfloat16), preferred_element_type=jnp.float32
        )
        m_ref[:, c0:c0 + cols] = m_new

    for qb in range(q_ref.shape[1] // cols):
        for blocks in range(1, pieces + 1):
            for diagonal in (False, True):
                hit = (t == diagonal_shard) if diagonal else (t != diagonal_shard)

                @pl.when(active & hit & (qb < q_blocks) & (key_blocks == blocks))
                def _():
                    step(qb, blocks * SUB, diagonal)


def attend(scalars, q, qpos, kpos, kv, steps, interpret=False):
    head_dim, q_rows = q.shape
    shards, kv_rows, slots = kv.shape
    cols = kpos.shape[1]
    kernel = functools.partial(attend_kernel, cols=cols, steps=steps)

    def fixed(i, sc):
        return (0, 0)

    def shard_of(i, sc):
        last = jnp.maximum(sc[1] - 1, 0)
        return (jnp.clip(sc[0] + jnp.minimum(i, last), 0, shards - 1), 0, 0)

    grid_spec = pltpu.PrefetchScalarGridSpec(
        num_scalar_prefetch=1,
        grid=(steps,),
        in_specs=[
            pl.BlockSpec((head_dim, q_rows), fixed),
            pl.BlockSpec((1, q_rows), fixed),
            pl.BlockSpec((slots, cols), fixed),
            pl.BlockSpec((None, SUB + head_dim, slots), shard_of),
        ],
        out_specs=pl.BlockSpec((head_dim + STATE_ROWS, q_rows), fixed),
    )
    return pl.pallas_call(
        kernel,
        grid_spec=grid_spec,
        out_shape=jax.ShapeDtypeStruct((head_dim + STATE_ROWS, q_rows), jnp.float32),
        compiler_params=pltpu.CompilerParams(dimension_semantics=("arbitrary",)),
        interpret=interpret,
    )(scalars, q, qpos, kpos, kv)


def merge(first, second):
    head_dim = first.shape[0] - STATE_ROWS
    acc_a, m_a, l_a = first[:head_dim], first[head_dim:head_dim + 1], first[head_dim + 1:head_dim + 2]
    acc_b, m_b, l_b = second[:head_dim], second[head_dim:head_dim + 1], second[head_dim + 1:head_dim + 2]
    m_a = jnp.where(l_a > 0.0, m_a, MASKED)
    m_b = jnp.where(l_b > 0.0, m_b, MASKED)
    m = jnp.maximum(m_a, m_b)
    scale_a = jnp.exp(m_a - m)
    scale_b = jnp.exp(m_b - m)
    return acc_a * scale_a + acc_b * scale_b, l_a * scale_a + l_b * scale_b


FLAG_ROWS = 16
EXTRA_OWN = 4


def pack_payload(key_rows, value_rows, live):
    slot_count = live.shape[0]
    head_dim = key_rows.shape[-1]
    keys = key_rows.reshape(slot_count // SUB, SUB, head_dim)
    keys = jnp.transpose(keys, (1, 0, 2)).reshape(SUB, slot_count)
    values = jnp.transpose(value_rows.reshape(slot_count, head_dim))
    flags = jnp.zeros((FLAG_ROWS, slot_count), jnp.bfloat16).at[0].set(live.astype(jnp.bfloat16))
    return jnp.concatenate([keys, values, flags], axis=0)


def ring_project(picked, weights, axis):
    size = lax.axis_size(axis)
    idx = lax.axis_index(axis)
    width = picked.shape[1]
    forward = [(i, (i + 1) % size) for i in range(size)]
    backward = [(i, (i - 1) % size) for i in range(size)]

    def partial(block, source):
        start = source * width
        return [
            jnp.dot(block, lax.dynamic_slice_in_dim(w, start, width, axis=0), preferred_element_type=jnp.float32)
            for w in weights
        ]

    sums = partial(picked, idx)
    ahead = picked
    behind = picked
    steps_behind = (size - 1) // 2
    for step in range(1, steps_behind + 1):
        ahead = lax.ppermute(ahead, axis, forward)
        behind = lax.ppermute(behind, axis, backward)
        for part in (partial(ahead, (idx - step) % size), partial(behind, (idx + step) % size)):
            sums = [s + p for s, p in zip(sums, part)]
    if size % 2 == 0:
        rows = picked.shape[0] // 2
        top = lax.ppermute(ahead[:rows], axis, forward)
        bottom = lax.ppermute(behind[rows:], axis, backward)
        part = partial(jnp.concatenate([top, bottom], axis=0), (idx + size // 2) % size)
        sums = [s + p for s, p in zip(sums, part)]
    return sums


def body(hidden_states, chosen, router_gate, w_query, w_key, w_value):
    seq_rows = hidden_states.shape[0]
    slot_count = chosen.shape[0]
    head_dim = HEAD_DIM
    query_width = w_query.shape[1]
    kv_width = w_key.shape[1]
    kv_local = kv_width // head_dim
    heads_local = query_width // head_dim
    group = heads_local // kv_local
    shards = lax.axis_size("ctx")
    live = chosen < seq_rows
    pad_mark = shards * seq_rows + 1
    position = jnp.where(live, lax.axis_index("ctx") * seq_rows + chosen, pad_mark)
    picked = hidden_states[jnp.minimum(chosen, seq_rows - 1)]
    gated = jnp.where(live, router_gate, 0.0)
    query_part, key_part, value_part = ring_project(picked, (w_query, w_key, w_value), "tp")
    queries = (
        rotate(query_part.reshape(slot_count, heads_local, head_dim), position) * head_dim ** (-0.5)
    ).astype(jnp.bfloat16)
    key_rows = rotate(key_part.reshape(slot_count, kv_local, head_dim), position).astype(
        jnp.bfloat16
    )
    value_rows = value_part.reshape(slot_count, kv_local, head_dim).astype(jnp.bfloat16)
    payload = pack_payload(key_rows, value_rows, live)
    payload = lax.all_gather(payload, "ctx", axis=0, tiled=True)
    blocks = payload.reshape(shards, payload.shape[0] // shards, slot_count)
    flag_row = blocks.shape[1] - FLAG_ROWS
    counts = jnp.sum(blocks[:, flag_row, :].astype(jnp.float32), axis=1).astype(jnp.int32)
    own = lax.axis_index("ctx")
    half = shards // 2
    partner = shards - 1 - own

    def live_blocks(count):
        return (count + (SUB - 1)) // SUB

    def scalars_of(first, count, q_blocks, diagonal):
        head = jnp.stack([first, count, q_blocks, diagonal]).astype(jnp.int32)
        return jnp.concatenate([head, counts])

    q_tiles = slot_count // SUB
    flat_q = jnp.transpose(
        queries.reshape(q_tiles, SUB, group, head_dim), (0, 2, 1, 3)
    ).reshape(slot_count * group, head_dim)
    own_q = jnp.transpose(flat_q)

    def per_column(values):
        spread = jnp.broadcast_to(values.reshape(q_tiles, 1, SUB), (q_tiles, group, SUB))
        return spread.reshape(1, slot_count * group)

    own_pos = jnp.broadcast_to(chosen[:, None], (slot_count, group * SUB))
    query_pos = per_column(chosen)
    guest_q = lax.ppermute(own_q, "ctx", [(j, shards - 1 - j) for j in range(half, shards)])
    guest_count = jnp.maximum(half - EXTRA_OWN - own, 0)
    guest_scalars = scalars_of(
        jnp.int32(0), guest_count, live_blocks(counts[partner]), jnp.int32(-1)
    )

    def guest_work(q):
        return attend(guest_scalars, q, query_pos, own_pos, blocks, half - EXTRA_OWN)

    def no_guest(q):
        return jnp.zeros((q.shape[0] + STATE_ROWS, q.shape[1]), jnp.float32)

    guest_state = lax.cond(guest_count > 0, guest_work, no_guest, guest_q)
    returned = lax.ppermute(guest_state, "ctx", [(j, shards - 1 - j) for j in range(half)])
    own_q, guest_state = lax.optimization_barrier((own_q, guest_state))
    own_first = jnp.maximum(own - (half - 1) - EXTRA_OWN, 0)
    own_scalars = scalars_of(
        own_first, own - own_first + 1, live_blocks(jnp.sum(live.astype(jnp.int32))), own
    )
    own_state = attend(own_scalars, own_q, query_pos, own_pos, blocks, half + EXTRA_OWN)
    acc, total = merge(own_state, returned)
    out = (acc / jnp.where(total > 0.0, total, 1.0)) * per_column(gated)
    out = jnp.transpose(out.astype(jnp.bfloat16))
    out = jnp.transpose(out.reshape(q_tiles, group, SUB, head_dim), (0, 2, 1, 3))
    return out.reshape(slot_count, query_width)


def solution(mesh):
    placed = (P("ctx", "tp"), P("ctx"), P("ctx"), P(None, "tp"), P(None, "tp"), P(None, "tp"))
    return jax.shard_map(
        body, mesh=mesh, in_specs=placed, out_specs=P("ctx", "tp"), check_vma=False
    )
```

```python
import functools
import math

import jax
import jax.numpy as jnp
from jax import lax
from jax.experimental import pallas as pl
from jax.experimental.pallas import tpu as pltpu
from jax.sharding import PartitionSpec as P

HEAD_DIM = 128


ROPE_BASE = 500000.0
MASKED = -1e30
SUB = 128
STATE_ROWS = 8


def rotate(values_in, position):
    half_dim = values_in.shape[-1] // 2
    frequency = jnp.exp(
        jnp.arange(half_dim, dtype=jnp.float32) * (-2.0 * math.log(ROPE_BASE) / values_in.shape[-1])
    )
    angles = position.astype(jnp.float32)[:, None] * frequency[None, :]
    cosine = jnp.cos(angles)[:, None, :]
    sine = jnp.sin(angles)[:, None, :]
    first = values_in[..., :half_dim]
    second = values_in[..., half_dim:]
    return jnp.concatenate(
        [first * cosine - second * sine, second * cosine + first * sine], axis=-1
    )


def attend_kernel(scalars, q_ref, qpos_ref, kpos_ref, kv_ref, state_ref, *, cols, steps):
    i = pl.program_id(0)
    first = scalars[0]
    active = i < scalars[1]
    q_blocks = scalars[2]
    diagonal_shard = scalars[3]
    t = first + i
    count = scalars[4 + jnp.minimum(t, scalars.shape[0] - 5)]
    key_blocks = (count + (SUB - 1)) // SUB
    head_dim = q_ref.shape[0]
    pieces = kv_ref.shape[1] // SUB

    acc_ref = state_ref.at[0:head_dim, :]
    m_ref = state_ref.at[head_dim:head_dim + 1, :]
    l_ref = state_ref.at[head_dim + 1:head_dim + 2, :]

    @pl.when(i == 0)
    def _():
        state_ref[...] = jnp.zeros(state_ref.shape, jnp.float32)
        m_ref[...] = jnp.full(m_ref.shape, MASKED, jnp.float32)

    def step(qb, width, diagonal):
        c0 = qb * cols
        q = q_ref[:, c0:c0 + cols]
        chunks = [
            jnp.dot(kv_ref[0:SUB, j * SUB:(j + 1) * SUB], q, preferred_element_type=jnp.float32)
            for j in range(width // SUB)
        ]
        if diagonal:
            masks = [kpos_ref[j * SUB:(j + 1) * SUB, :] <= qpos_ref[:, c0:c0 + cols] for j in range(len(chunks))]
        else:
            last = lax.broadcasted_iota(jnp.int32, chunks[-1].shape, 0) + (width - SUB) < count
            masks = [None] * (len(chunks) - 1) + [last]
        m_prev = m_ref[:, c0:c0 + cols]
        m_new = m_prev
        for chunk, mask in zip(chunks, masks):
            kept = chunk if mask is None else jnp.where(mask, chunk, MASKED)
            m_new = jnp.maximum(m_new, jnp.max(kept, axis=0, keepdims=True))
        alpha = jnp.exp(m_prev - m_new)
        weights = []
        for chunk, mask in zip(chunks, masks):
            w = jnp.exp(chunk - m_new)
            weights.append(w if mask is None else jnp.where(mask, w, 0.0))
        p = jnp.concatenate(weights, axis=0)
        l_ref[:, c0:c0 + cols] = alpha * l_ref[:, c0:c0 + cols] + jnp.sum(p, axis=0, keepdims=True)
        acc_ref[:, c0:c0 + cols] = alpha * acc_ref[:, c0:c0 + cols] + jnp.dot(
            kv_ref[SUB:SUB + head_dim, 0:width], p.astype(jnp.bfloat16), preferred_element_type=jnp.float32
        )
        m_ref[:, c0:c0 + cols] = m_new

    for qb in range(q_ref.shape[1] // cols):
        for blocks in range(1, pieces + 1):
            for diagonal in (False, True):
                hit = (t == diagonal_shard) if diagonal else (t != diagonal_shard)

                @pl.when(active & hit & (qb < q_blocks) & (key_blocks == blocks))
                def _():
                    step(qb, blocks * SUB, diagonal)


def attend(scalars, q, qpos, kpos, kv, steps, interpret=False):
    head_dim, q_rows = q.shape
    shards, kv_rows, slots = kv.shape
    cols = kpos.shape[1]
    kernel = functools.partial(attend_kernel, cols=cols, steps=steps)

    def fixed(i, sc):
        return (0, 0)

    def shard_of(i, sc):
        last = jnp.maximum(sc[1] - 1, 0)
        return (jnp.clip(sc[0] + jnp.minimum(i, last), 0, shards - 1), 0, 0)

    grid_spec = pltpu.PrefetchScalarGridSpec(
        num_scalar_prefetch=1,
        grid=(steps,),
        in_specs=[
            pl.BlockSpec((head_dim, q_rows), fixed),
            pl.BlockSpec((1, q_rows), fixed),
            pl.BlockSpec((slots, cols), fixed),
            pl.BlockSpec((None, SUB + head_dim, slots), shard_of),
        ],
        out_specs=pl.BlockSpec((head_dim + STATE_ROWS, q_rows), fixed),
    )
    return pl.pallas_call(
        kernel,
        grid_spec=grid_spec,
        out_shape=jax.ShapeDtypeStruct((head_dim + STATE_ROWS, q_rows), jnp.float32),
        compiler_params=pltpu.CompilerParams(dimension_semantics=("arbitrary",)),
        interpret=interpret,
    )(scalars, q, qpos, kpos, kv)


def merge(first, second):
    head_dim = first.shape[0] - STATE_ROWS
    acc_a, m_a, l_a = first[:head_dim], first[head_dim:head_dim + 1], first[head_dim + 1:head_dim + 2]
    acc_b, m_b, l_b = second[:head_dim], second[head_dim:head_dim + 1], second[head_dim + 1:head_dim + 2]
    m_a = jnp.where(l_a > 0.0, m_a, MASKED)
    m_b = jnp.where(l_b > 0.0, m_b, MASKED)
    m = jnp.maximum(m_a, m_b)
    scale_a = jnp.exp(m_a - m)
    scale_b = jnp.exp(m_b - m)
    return acc_a * scale_a + acc_b * scale_b, l_a * scale_a + l_b * scale_b


FLAG_ROWS = 16
EXTRA_OWN = 2


def pack_payload(key_rows, value_rows, live):
    slot_count = live.shape[0]
    head_dim = key_rows.shape[-1]
    keys = key_rows.reshape(slot_count // SUB, SUB, head_dim)
    keys = jnp.transpose(keys, (1, 0, 2)).reshape(SUB, slot_count)
    values = jnp.transpose(value_rows.reshape(slot_count, head_dim))
    flags = jnp.zeros((FLAG_ROWS, slot_count), jnp.bfloat16).at[0].set(live.astype(jnp.bfloat16))
    return jnp.concatenate([keys, values, flags], axis=0)


def ring_project(picked, weights, axis):
    size = lax.axis_size(axis)
    idx = lax.axis_index(axis)
    width = picked.shape[1]
    forward = [(i, (i + 1) % size) for i in range(size)]
    backward = [(i, (i - 1) % size) for i in range(size)]

    def partial(block, source):
        start = source * width
        return [
            jnp.dot(block, lax.dynamic_slice_in_dim(w, start, width, axis=0), preferred_element_type=jnp.float32)
            for w in weights
        ]

    sums = partial(picked, idx)
    ahead = picked
    behind = picked
    steps_behind = (size - 1) // 2
    for step in range(1, steps_behind + 1):
        ahead = lax.ppermute(ahead, axis, forward)
        behind = lax.ppermute(behind, axis, backward)
        for part in (partial(ahead, (idx - step) % size), partial(behind, (idx + step) % size)):
            sums = [s + p for s, p in zip(sums, part)]
    if size % 2 == 0:
        rows = picked.shape[0] // 2
        top = lax.ppermute(ahead[:rows], axis, forward)
        bottom = lax.ppermute(behind[rows:], axis, backward)
        part = partial(jnp.concatenate([top, bottom], axis=0), (idx + size // 2) % size)
        sums = [s + p for s, p in zip(sums, part)]
    return sums


def body(hidden_states, chosen, router_gate, w_query, w_key, w_value):
    seq_rows = hidden_states.shape[0]
    slot_count = chosen.shape[0]
    head_dim = HEAD_DIM
    query_width = w_query.shape[1]
    kv_width = w_key.shape[1]
    kv_local = kv_width // head_dim
    heads_local = query_width // head_dim
    group = heads_local // kv_local
    shards = lax.axis_size("ctx")
    live = chosen < seq_rows
    pad_mark = shards * seq_rows + 1
    position = jnp.where(live, lax.axis_index("ctx") * seq_rows + chosen, pad_mark)
    picked = hidden_states[jnp.minimum(chosen, seq_rows - 1)]
    gated = jnp.where(live, router_gate, 0.0)
    query_part, key_part, value_part = ring_project(picked, (w_query, w_key, w_value), "tp")
    queries = (
        rotate(query_part.reshape(slot_count, heads_local, head_dim), position) * head_dim ** (-0.5)
    ).astype(jnp.bfloat16)
    key_rows = rotate(key_part.reshape(slot_count, kv_local, head_dim), position).astype(
        jnp.bfloat16
    )
    value_rows = value_part.reshape(slot_count, kv_local, head_dim).astype(jnp.bfloat16)
    payload = pack_payload(key_rows, value_rows, live)
    payload = lax.all_gather(payload, "ctx", axis=0, tiled=True)
    blocks = payload.reshape(shards, payload.shape[0] // shards, slot_count)
    flag_row = blocks.shape[1] - FLAG_ROWS
    counts = jnp.sum(blocks[:, flag_row, :].astype(jnp.float32), axis=1).astype(jnp.int32)
    own = lax.axis_index("ctx")
    half = shards // 2
    partner = shards - 1 - own

    def live_blocks(count):
        return (count + (SUB - 1)) // SUB

    def scalars_of(first, count, q_blocks, diagonal):
        head = jnp.stack([first, count, q_blocks, diagonal]).astype(jnp.int32)
        return jnp.concatenate([head, counts])

    q_tiles = slot_count // SUB
    flat_q = jnp.transpose(
        queries.reshape(q_tiles, SUB, group, head_dim), (0, 2, 1, 3)
    ).reshape(slot_count * group, head_dim)
    own_q = jnp.transpose(flat_q)

    def per_column(values):
        spread = jnp.broadcast_to(values.reshape(q_tiles, 1, SUB), (q_tiles, group, SUB))
        return spread.reshape(1, slot_count * group)

    own_pos = jnp.broadcast_to(chosen[:, None], (slot_count, group * SUB))
    query_pos = per_column(chosen)
    guest_q = lax.ppermute(own_q, "ctx", [(j, shards - 1 - j) for j in range(half, shards)])
    guest_count = jnp.maximum(half - EXTRA_OWN - own, 0)
    guest_scalars = scalars_of(
        jnp.int32(0), guest_count, live_blocks(counts[partner]), jnp.int32(-1)
    )

    def guest_work(q):
        return attend(guest_scalars, q, query_pos, own_pos, blocks, half - EXTRA_OWN)

    def no_guest(q):
        return jnp.zeros((q.shape[0] + STATE_ROWS, q.shape[1]), jnp.float32)

    guest_state = lax.cond(guest_count > 0, guest_work, no_guest, guest_q)
    returned = lax.ppermute(guest_state, "ctx", [(j, shards - 1 - j) for j in range(half)])
    own_q, guest_state = lax.optimization_barrier((own_q, guest_state))
    own_first = jnp.maximum(own - (half - 1) - EXTRA_OWN, 0)
    own_scalars = scalars_of(
        own_first, own - own_first + 1, live_blocks(jnp.sum(live.astype(jnp.int32))), own
    )
    own_state = attend(own_scalars, own_q, query_pos, own_pos, blocks, half + EXTRA_OWN)
    acc, total = merge(own_state, returned)
    out = (acc / jnp.where(total > 0.0, total, 1.0)) * per_column(gated)
    out = jnp.transpose(out.astype(jnp.bfloat16))
    out = jnp.transpose(out.reshape(q_tiles, group, SUB, head_dim), (0, 2, 1, 3))
    return out.reshape(slot_count, query_width)


def solution(mesh):
    placed = (P("ctx", "tp"), P("ctx"), P("ctx"), P(None, "tp"), P(None, "tp"), P(None, "tp"))
    return jax.shard_map(
        body, mesh=mesh, in_specs=placed, out_specs=P("ctx", "tp"), check_vma=False
    )
```

```python
import functools
import math

import jax
import jax.numpy as jnp
from jax import lax
from jax.experimental import pallas as pl
from jax.experimental.pallas import tpu as pltpu
from jax.sharding import PartitionSpec as P

HEAD_DIM = 128


ROPE_BASE = 500000.0
MASKED = -1e30
SUB = 128
STATE_ROWS = 8


def rotate(values_in, position):
    half_dim = values_in.shape[-1] // 2
    frequency = jnp.exp(
        jnp.arange(half_dim, dtype=jnp.float32) * (-2.0 * math.log(ROPE_BASE) / values_in.shape[-1])
    )
    angles = position.astype(jnp.float32)[:, None] * frequency[None, :]
    cosine = jnp.cos(angles)[:, None, :]
    sine = jnp.sin(angles)[:, None, :]
    first = values_in[..., :half_dim]
    second = values_in[..., half_dim:]
    return jnp.concatenate(
        [first * cosine - second * sine, second * cosine + first * sine], axis=-1
    )


def attend_kernel(scalars, q_ref, qpos_ref, kpos_ref, kv_ref, init_ref, state_ref, *, cols, steps):
    i = pl.program_id(0)
    first = scalars[0]
    active = i < scalars[1]
    q_blocks = scalars[2]
    diagonal_shard = scalars[3]
    t = first + i
    count = scalars[4 + jnp.minimum(t, scalars.shape[0] - 5)]
    key_blocks = (count + (SUB - 1)) // SUB
    head_dim = q_ref.shape[0]
    pieces = kv_ref.shape[1] // SUB

    acc_ref = state_ref.at[0:head_dim, :]
    m_ref = state_ref.at[head_dim:head_dim + 1, :]
    l_ref = state_ref.at[head_dim + 1:head_dim + 2, :]

    @pl.when(i == 0)
    def _():
        state_ref[...] = init_ref[...]

    def step(qb, width, diagonal):
        c0 = qb * cols
        q = q_ref[:, c0:c0 + cols]
        chunks = [
            jnp.dot(kv_ref[0:SUB, j * SUB:(j + 1) * SUB], q, preferred_element_type=jnp.float32)
            for j in range(width // SUB)
        ]
        if diagonal:
            masks = [kpos_ref[j * SUB:(j + 1) * SUB, :] <= qpos_ref[:, c0:c0 + cols] for j in range(len(chunks))]
        else:
            last = lax.broadcasted_iota(jnp.int32, chunks[-1].shape, 0) + (width - SUB) < count
            masks = [None] * (len(chunks) - 1) + [last]
        m_prev = m_ref[:, c0:c0 + cols]
        m_new = m_prev
        for chunk, mask in zip(chunks, masks):
            kept = chunk if mask is None else jnp.where(mask, chunk, MASKED)
            m_new = jnp.maximum(m_new, jnp.max(kept, axis=0, keepdims=True))
        alpha = jnp.exp(m_prev - m_new)
        weights = []
        for chunk, mask in zip(chunks, masks):
            w = jnp.exp(chunk - m_new)
            weights.append(w if mask is None else jnp.where(mask, w, 0.0))
        p = jnp.concatenate(weights, axis=0)
        l_ref[:, c0:c0 + cols] = alpha * l_ref[:, c0:c0 + cols] + jnp.sum(p, axis=0, keepdims=True)
        acc_ref[:, c0:c0 + cols] = alpha * acc_ref[:, c0:c0 + cols] + jnp.dot(
            kv_ref[SUB:SUB + head_dim, 0:width], p.astype(jnp.bfloat16), preferred_element_type=jnp.float32
        )
        m_ref[:, c0:c0 + cols] = m_new

    for qb in range(q_ref.shape[1] // cols):
        for blocks in range(1, pieces + 1):
            for diagonal in (False, True):
                hit = (t == diagonal_shard) if diagonal else (t != diagonal_shard)

                @pl.when(active & hit & (qb < q_blocks) & (key_blocks == blocks))
                def _():
                    step(qb, blocks * SUB, diagonal)


def attend(scalars, q, qpos, kpos, kv, init, steps, interpret=False):
    head_dim, q_rows = q.shape
    shards, kv_rows, slots = kv.shape
    cols = kpos.shape[1]
    kernel = functools.partial(attend_kernel, cols=cols, steps=steps)

    def fixed(i, sc):
        return (0, 0)

    def shard_of(i, sc):
        last = jnp.maximum(sc[1] - 1, 0)
        return (jnp.clip(sc[0] + jnp.minimum(i, last), 0, shards - 1), 0, 0)

    grid_spec = pltpu.PrefetchScalarGridSpec(
        num_scalar_prefetch=1,
        grid=(steps,),
        in_specs=[
            pl.BlockSpec((head_dim, q_rows), fixed),
            pl.BlockSpec((1, q_rows), fixed),
            pl.BlockSpec((slots, cols), fixed),
            pl.BlockSpec((None, SUB + head_dim, slots), shard_of),
            pl.BlockSpec((head_dim + STATE_ROWS, q_rows), fixed),
        ],
        out_specs=pl.BlockSpec((head_dim + STATE_ROWS, q_rows), fixed),
    )
    return pl.pallas_call(
        kernel,
        grid_spec=grid_spec,
        out_shape=jax.ShapeDtypeStruct((head_dim + STATE_ROWS, q_rows), jnp.float32),
        compiler_params=pltpu.CompilerParams(dimension_semantics=("arbitrary",)),
        interpret=interpret,
    )(scalars, q, qpos, kpos, kv, init)


def empty_state(q):
    head_dim, q_rows = q.shape
    state = jnp.zeros((head_dim + STATE_ROWS, q_rows), jnp.float32)
    return state.at[head_dim].set(MASKED)


def merge(first, second):
    head_dim = first.shape[0] - STATE_ROWS
    acc_a, m_a, l_a = first[:head_dim], first[head_dim:head_dim + 1], first[head_dim + 1:head_dim + 2]
    acc_b, m_b, l_b = second[:head_dim], second[head_dim:head_dim + 1], second[head_dim + 1:head_dim + 2]
    m_a = jnp.where(l_a > 0.0, m_a, MASKED)
    m_b = jnp.where(l_b > 0.0, m_b, MASKED)
    m = jnp.maximum(m_a, m_b)
    scale_a = jnp.exp(m_a - m)
    scale_b = jnp.exp(m_b - m)
    return acc_a * scale_a + acc_b * scale_b, l_a * scale_a + l_b * scale_b


FLAG_ROWS = 16
EXTRA_OWN = 2


def pack_payload(key_rows, value_rows, live):
    slot_count = live.shape[0]
    head_dim = key_rows.shape[-1]
    keys = key_rows.reshape(slot_count // SUB, SUB, head_dim)
    keys = jnp.transpose(keys, (1, 0, 2)).reshape(SUB, slot_count)
    values = jnp.transpose(value_rows.reshape(slot_count, head_dim))
    flags = jnp.zeros((FLAG_ROWS, slot_count), jnp.bfloat16).at[0].set(live.astype(jnp.bfloat16))
    return jnp.concatenate([keys, values, flags], axis=0)


def ring_project(picked, weights, axis):
    size = lax.axis_size(axis)
    idx = lax.axis_index(axis)
    width = picked.shape[1]
    forward = [(i, (i + 1) % size) for i in range(size)]
    backward = [(i, (i - 1) % size) for i in range(size)]

    def partial(block, source):
        start = source * width
        return [
            jnp.dot(block, lax.dynamic_slice_in_dim(w, start, width, axis=0), preferred_element_type=jnp.float32)
            for w in weights
        ]

    sums = partial(picked, idx)
    ahead = picked
    behind = picked
    steps_behind = (size - 1) // 2
    for step in range(1, steps_behind + 1):
        ahead = lax.ppermute(ahead, axis, forward)
        behind = lax.ppermute(behind, axis, backward)
        for part in (partial(ahead, (idx - step) % size), partial(behind, (idx + step) % size)):
            sums = [s + p for s, p in zip(sums, part)]
    if size % 2 == 0:
        rows = picked.shape[0] // 2
        top = lax.ppermute(ahead[:rows], axis, forward)
        bottom = lax.ppermute(behind[rows:], axis, backward)
        part = partial(jnp.concatenate([top, bottom], axis=0), (idx + size // 2) % size)
        sums = [s + p for s, p in zip(sums, part)]
    return sums


def body(hidden_states, chosen, router_gate, w_query, w_key, w_value):
    seq_rows = hidden_states.shape[0]
    slot_count = chosen.shape[0]
    head_dim = HEAD_DIM
    query_width = w_query.shape[1]
    kv_width = w_key.shape[1]
    kv_local = kv_width // head_dim
    heads_local = query_width // head_dim
    group = heads_local // kv_local
    shards = lax.axis_size("ctx")
    live = chosen < seq_rows
    pad_mark = shards * seq_rows + 1
    position = jnp.where(live, lax.axis_index("ctx") * seq_rows + chosen, pad_mark)
    picked = hidden_states[jnp.minimum(chosen, seq_rows - 1)]
    gated = jnp.where(live, router_gate, 0.0)
    query_part, key_part, value_part = ring_project(picked, (w_query, w_key, w_value), "tp")
    queries = (
        rotate(query_part.reshape(slot_count, heads_local, head_dim), position) * head_dim ** (-0.5)
    ).astype(jnp.bfloat16)
    key_rows = rotate(key_part.reshape(slot_count, kv_local, head_dim), position).astype(
        jnp.bfloat16
    )
    value_rows = value_part.reshape(slot_count, kv_local, head_dim).astype(jnp.bfloat16)
    payload = pack_payload(key_rows, value_rows, live)
    local = payload
    payload = lax.all_gather(payload, "ctx", axis=0, tiled=True)
    blocks = payload.reshape(shards, payload.shape[0] // shards, slot_count)
    flag_row = blocks.shape[1] - FLAG_ROWS
    counts = jnp.sum(blocks[:, flag_row, :].astype(jnp.float32), axis=1).astype(jnp.int32)
    own = lax.axis_index("ctx")
    half = shards // 2
    partner = shards - 1 - own

    def live_blocks(count):
        return (count + (SUB - 1)) // SUB

    def scalars_of(first, count, q_blocks, diagonal):
        head = jnp.stack([first, count, q_blocks, diagonal]).astype(jnp.int32)
        return jnp.concatenate([head, counts])

    q_tiles = slot_count // SUB
    flat_q = jnp.transpose(
        queries.reshape(q_tiles, SUB, group, head_dim), (0, 2, 1, 3)
    ).reshape(slot_count * group, head_dim)
    own_q = jnp.transpose(flat_q)

    def per_column(values):
        spread = jnp.broadcast_to(values.reshape(q_tiles, 1, SUB), (q_tiles, group, SUB))
        return spread.reshape(1, slot_count * group)

    own_pos = jnp.broadcast_to(chosen[:, None], (slot_count, group * SUB))
    query_pos = per_column(chosen)
    own_count = jnp.sum(live.astype(jnp.int32))
    own_blocks = live_blocks(own_count)
    diagonal_scalars = jnp.stack([0, 1, own_blocks, 0, own_count]).astype(jnp.int32)
    diagonal_state = attend(
        diagonal_scalars, own_q, query_pos, own_pos, local[None], empty_state(own_q), 1
    )
    sent_q, diagonal_state = lax.optimization_barrier((own_q, diagonal_state))
    guest_q = lax.ppermute(sent_q, "ctx", [(j, shards - 1 - j) for j in range(half, shards)])
    guest_count = jnp.maximum(half - EXTRA_OWN - own, 0)
    guest_scalars = scalars_of(
        jnp.int32(0), guest_count, live_blocks(counts[partner]), jnp.int32(-1)
    )

    def guest_work(q):
        return attend(guest_scalars, q, query_pos, own_pos, blocks, empty_state(q), half - EXTRA_OWN)

    def no_guest(q):
        return jnp.zeros((q.shape[0] + STATE_ROWS, q.shape[1]), jnp.float32)

    guest_state = lax.cond(guest_count > 0, guest_work, no_guest, guest_q)
    returned = lax.ppermute(guest_state, "ctx", [(j, shards - 1 - j) for j in range(half)])
    own_q, guest_state = lax.optimization_barrier((own_q, guest_state))
    own_first = jnp.maximum(own - (half - 1) - EXTRA_OWN, 0)
    own_scalars = scalars_of(
        own_first, own - own_first, own_blocks, jnp.int32(-1)
    )
    own_state = attend(own_scalars, own_q, query_pos, own_pos, blocks, diagonal_state, half + EXTRA_OWN - 1)
    acc, total = merge(own_state, returned)
    out = (acc / jnp.where(total > 0.0, total, 1.0)) * per_column(gated)
    out = jnp.transpose(out.astype(jnp.bfloat16))
    out = jnp.transpose(out.reshape(q_tiles, group, SUB, head_dim), (0, 2, 1, 3))
    return out.reshape(slot_count, query_width)


def solution(mesh):
    placed = (P("ctx", "tp"), P("ctx"), P("ctx"), P(None, "tp"), P(None, "tp"), P(None, "tp"))
    return jax.shard_map(
        body, mesh=mesh, in_specs=placed, out_specs=P("ctx", "tp"), check_vma=False
    )
```

```python
import functools
import math

import jax
import jax.numpy as jnp
from jax import lax
from jax.experimental import pallas as pl
from jax.experimental.pallas import tpu as pltpu
from jax.sharding import PartitionSpec as P

HEAD_DIM = 128


ROPE_BASE = 500000.0
MASKED = -1e30
SUB = 128
STATE_ROWS = 8


def rotate(values_in, position):
    half_dim = values_in.shape[-1] // 2
    frequency = jnp.exp(
        jnp.arange(half_dim, dtype=jnp.float32) * (-2.0 * math.log(ROPE_BASE) / values_in.shape[-1])
    )
    angles = position.astype(jnp.float32)[:, None] * frequency[None, :]
    cosine = jnp.cos(angles)[:, None, :]
    sine = jnp.sin(angles)[:, None, :]
    first = values_in[..., :half_dim]
    second = values_in[..., half_dim:]
    return jnp.concatenate(
        [first * cosine - second * sine, second * cosine + first * sine], axis=-1
    )


def attend_kernel(scalars, q_ref, qpos_ref, kpos_ref, kv_ref, state_ref, *, cols, steps):
    i = pl.program_id(0)
    first = scalars[0]
    active = i < scalars[1]
    q_blocks = scalars[2]
    diagonal_shard = scalars[3]
    t = first + i
    count = scalars[4 + jnp.minimum(t, scalars.shape[0] - 5)]
    key_blocks = (count + (SUB - 1)) // SUB
    head_dim = q_ref.shape[0]
    pieces = kv_ref.shape[1] // SUB

    acc_ref = state_ref.at[0:head_dim, :]
    m_ref = state_ref.at[head_dim:head_dim + 1, :]
    l_ref = state_ref.at[head_dim + 1:head_dim + 2, :]

    @pl.when(i == 0)
    def _():
        state_ref[...] = jnp.zeros(state_ref.shape, jnp.float32)
        m_ref[...] = jnp.full(m_ref.shape, MASKED, jnp.float32)

    def step(qb, width, diagonal):
        c0 = qb * cols
        q = q_ref[:, c0:c0 + cols]
        chunks = [
            jnp.dot(kv_ref[0:SUB, j * SUB:(j + 1) * SUB], q, preferred_element_type=jnp.float32)
            for j in range(width // SUB)
        ]
        if diagonal:
            masks = [kpos_ref[j * SUB:(j + 1) * SUB, :] <= qpos_ref[:, c0:c0 + cols] for j in range(len(chunks))]
        else:
            last = lax.broadcasted_iota(jnp.int32, chunks[-1].shape, 0) + (width - SUB) < count
            masks = [None] * (len(chunks) - 1) + [last]
        m_prev = m_ref[:, c0:c0 + cols]
        m_new = m_prev
        for chunk, mask in zip(chunks, masks):
            kept = chunk if mask is None else jnp.where(mask, chunk, MASKED)
            m_new = jnp.maximum(m_new, jnp.max(kept, axis=0, keepdims=True))
        alpha = jnp.exp(m_prev - m_new)
        weights = []
        for chunk, mask in zip(chunks, masks):
            w = jnp.exp(chunk - m_new)
            weights.append(w if mask is None else jnp.where(mask, w, 0.0))
        p = jnp.concatenate(weights, axis=0)
        l_ref[:, c0:c0 + cols] = alpha * l_ref[:, c0:c0 + cols] + jnp.sum(p, axis=0, keepdims=True)
        acc_ref[:, c0:c0 + cols] = alpha * acc_ref[:, c0:c0 + cols] + jnp.dot(
            kv_ref[SUB:SUB + head_dim, 0:width], p.astype(jnp.bfloat16), preferred_element_type=jnp.float32
        )
        m_ref[:, c0:c0 + cols] = m_new

    for qb in range(q_ref.shape[1] // cols):
        for blocks in range(1, pieces + 1):
            for diagonal in (False, True):
                hit = (t == diagonal_shard) if diagonal else (t != diagonal_shard)

                @pl.when(active & hit & (qb < q_blocks) & (key_blocks == blocks))
                def _():
                    step(qb, blocks * SUB, diagonal)


def attend(scalars, q, qpos, kpos, kv, steps, interpret=False):
    head_dim, q_rows = q.shape
    shards, kv_rows, slots = kv.shape
    cols = kpos.shape[1]
    kernel = functools.partial(attend_kernel, cols=cols, steps=steps)

    def fixed(i, sc):
        return (0, 0)

    def shard_of(i, sc):
        last = jnp.maximum(sc[1] - 1, 0)
        return (jnp.clip(sc[0] + jnp.minimum(i, last), 0, shards - 1), 0, 0)

    grid_spec = pltpu.PrefetchScalarGridSpec(
        num_scalar_prefetch=1,
        grid=(steps,),
        in_specs=[
            pl.BlockSpec((head_dim, q_rows), fixed),
            pl.BlockSpec((1, q_rows), fixed),
            pl.BlockSpec((slots, cols), fixed),
            pl.BlockSpec((None, SUB + head_dim, slots), shard_of),
        ],
        out_specs=pl.BlockSpec((head_dim + STATE_ROWS, q_rows), fixed),
    )
    return pl.pallas_call(
        kernel,
        grid_spec=grid_spec,
        out_shape=jax.ShapeDtypeStruct((head_dim + STATE_ROWS, q_rows), jnp.float32),
        compiler_params=pltpu.CompilerParams(dimension_semantics=("arbitrary",)),
        interpret=interpret,
    )(scalars, q, qpos, kpos, kv)


def merge(first, second):
    head_dim = first.shape[0] - STATE_ROWS
    acc_a, m_a, l_a = first[:head_dim], first[head_dim:head_dim + 1], first[head_dim + 1:head_dim + 2]
    acc_b, m_b, l_b = second[:head_dim], second[head_dim:head_dim + 1], second[head_dim + 1:head_dim + 2]
    m_a = jnp.where(l_a > 0.0, m_a, MASKED)
    m_b = jnp.where(l_b > 0.0, m_b, MASKED)
    m = jnp.maximum(m_a, m_b)
    scale_a = jnp.exp(m_a - m)
    scale_b = jnp.exp(m_b - m)
    return acc_a * scale_a + acc_b * scale_b, l_a * scale_a + l_b * scale_b


FLAG_ROWS = 16
EXTRA_OWN = 2


def pack_payload(key_rows, value_rows, live):
    slot_count = live.shape[0]
    head_dim = key_rows.shape[-1]
    keys = key_rows.reshape(slot_count // SUB, SUB, head_dim)
    keys = jnp.transpose(keys, (1, 0, 2)).reshape(SUB, slot_count)
    values = jnp.transpose(value_rows.reshape(slot_count, head_dim))
    flags = jnp.zeros((FLAG_ROWS, slot_count), jnp.bfloat16).at[0].set(live.astype(jnp.bfloat16))
    return jnp.concatenate([keys, values, flags], axis=0)


def ring_project(picked, weights, axis):
    size = lax.axis_size(axis)
    idx = lax.axis_index(axis)
    width = picked.shape[1]
    forward = [(i, (i + 1) % size) for i in range(size)]
    backward = [(i, (i - 1) % size) for i in range(size)]

    def partial(block, source):
        start = source * width
        return [
            jnp.dot(block, lax.dynamic_slice_in_dim(w, start, width, axis=0), preferred_element_type=jnp.float32)
            for w in weights
        ]

    sums = partial(picked, idx)
    ahead = picked
    behind = picked
    steps_behind = (size - 1) // 2
    for step in range(1, steps_behind + 1):
        ahead = lax.ppermute(ahead, axis, forward)
        behind = lax.ppermute(behind, axis, backward)
        for part in (partial(ahead, (idx - step) % size), partial(behind, (idx + step) % size)):
            sums = [s + p for s, p in zip(sums, part)]
    if size % 2 == 0:
        rows = picked.shape[0] // 2
        top = lax.ppermute(ahead[:rows], axis, forward)
        bottom = lax.ppermute(behind[rows:], axis, backward)
        part = partial(jnp.concatenate([top, bottom], axis=0), (idx + size // 2) % size)
        sums = [s + p for s, p in zip(sums, part)]
    return sums


def body(hidden_states, chosen, router_gate, w_query, w_key, w_value):
    seq_rows = hidden_states.shape[0]
    slot_count = chosen.shape[0]
    head_dim = HEAD_DIM
    query_width = w_query.shape[1]
    kv_width = w_key.shape[1]
    kv_local = kv_width // head_dim
    heads_local = query_width // head_dim
    group = heads_local // kv_local
    shards = lax.axis_size("ctx")
    live = chosen < seq_rows
    pad_mark = shards * seq_rows + 1
    position = jnp.where(live, lax.axis_index("ctx") * seq_rows + chosen, pad_mark)
    picked = hidden_states[jnp.minimum(chosen, seq_rows - 1)]
    gated = jnp.where(live, router_gate, 0.0)
    query_part, key_part, value_part = ring_project(picked, (w_query, w_key, w_value), "tp")
    queries = (
        rotate(query_part.reshape(slot_count, heads_local, head_dim), position) * head_dim ** (-0.5)
    ).astype(jnp.bfloat16)
    key_rows = rotate(key_part.reshape(slot_count, kv_local, head_dim), position).astype(
        jnp.bfloat16
    )
    value_rows = value_part.reshape(slot_count, kv_local, head_dim).astype(jnp.bfloat16)
    payload = pack_payload(key_rows, value_rows, live)
    payload = lax.all_gather(payload, "ctx", axis=0, tiled=True)
    blocks = payload.reshape(shards, payload.shape[0] // shards, slot_count)
    flag_row = blocks.shape[1] - FLAG_ROWS
    counts = jnp.sum(blocks[:, flag_row, :].astype(jnp.float32), axis=1).astype(jnp.int32)
    own = lax.axis_index("ctx")
    half = shards // 2
    partner = shards - 1 - own

    def live_blocks(count):
        return (count + (SUB - 1)) // SUB

    def scalars_of(first, count, q_blocks, diagonal):
        head = jnp.stack([first, count, q_blocks, diagonal]).astype(jnp.int32)
        return jnp.concatenate([head, counts])

    q_tiles = slot_count // SUB
    flat_q = jnp.transpose(
        queries.reshape(q_tiles, SUB, group, head_dim), (0, 2, 1, 3)
    ).reshape(slot_count * group, head_dim)
    own_q = jnp.transpose(flat_q)

    def per_column(values):
        spread = jnp.broadcast_to(values.reshape(q_tiles, 1, SUB), (q_tiles, group, SUB))
        return spread.reshape(1, slot_count * group)

    own_pos = jnp.broadcast_to(chosen[:, None], (slot_count, group * SUB))
    query_pos = per_column(chosen)
    guest_q = lax.ppermute(own_q, "ctx", [(j, shards - 1 - j) for j in range(half, shards)])
    guest_count = jnp.maximum(half - EXTRA_OWN - own, 0)
    guest_scalars = scalars_of(
        jnp.int32(0), guest_count, live_blocks(counts[partner]), jnp.int32(-1)
    )

    def guest_work(q):
        return attend(guest_scalars, q, query_pos, own_pos, blocks, half - EXTRA_OWN)

    def no_guest(q):
        return jnp.zeros((q.shape[0] + STATE_ROWS, q.shape[1]), jnp.float32)

    own_first = jnp.maximum(own - (half - 1) - EXTRA_OWN, 0)
    own_scalars = scalars_of(
        own_first, own - own_first + 1, live_blocks(jnp.sum(live.astype(jnp.int32))), own
    )
    guest_q, own_scalars = lax.optimization_barrier((guest_q, own_scalars))
    guest_state = lax.cond(guest_count > 0, guest_work, no_guest, guest_q)
    returned = lax.ppermute(guest_state, "ctx", [(j, shards - 1 - j) for j in range(half)])
    own_q, guest_state = lax.optimization_barrier((own_q, guest_state))
    own_state = attend(own_scalars, own_q, query_pos, own_pos, blocks, half + EXTRA_OWN)
    acc, total = merge(own_state, returned)
    out = (acc / jnp.where(total > 0.0, total, 1.0)) * per_column(gated)
    out = jnp.transpose(out.astype(jnp.bfloat16))
    out = jnp.transpose(out.reshape(q_tiles, group, SUB, head_dim), (0, 2, 1, 3))
    return out.reshape(slot_count, query_width)


def solution(mesh):
    placed = (P("ctx", "tp"), P("ctx"), P("ctx"), P(None, "tp"), P(None, "tp"), P(None, "tp"))
    return jax.shard_map(
        body, mesh=mesh, in_specs=placed, out_specs=P("ctx", "tp"), check_vma=False
    )
```
